32 devices in a mesh: groups: 2 (over x), tm: 16 (over z, y, core).
Axes of the slice: x: 2, y: 2, z: 4, core: 2. Of those that a mesh axis runs over, the one named last changes fastest.
Arguments:
- hyper: float32 [6], P('groups'), parts along dimension 0, may hold values from 0.5 to 0.9
- spatial_prec: float32 [768, 768], replicated, as said below
- part_lengths: int32 [32], P('groups'), parts along dimension 0, may hold values from 1 to 2, as said below
- reading_index: int32 [4, 32, 1024], P(None, ('groups', 'tm')), parts along dimension 1, may hold values from 0 to 767, as said below
- reading_value: float32 [4, 32, 1024], P(None, ('groups', 'tm')), parts along dimension 1, as said below
- reading_cov: float32 [16, 32, 1024], P(None, ('groups', 'tm')), parts along dimension 1, may hold values from -0.1875 to 0.1875
Outputs:
- sep_block: float32 [32, 768, 768], P(('groups', 'tm')), parts along dimension 0
- fill_block: float32 [32, 768, 768], P(('groups', 'tm')), parts along dimension 0
- sep_border: float32 [32, 16, 768], P(('groups', 'tm')), parts along dimension 0
- tip: float32 [32, 16], P('groups'), parts along dimension 0
The draws below stay inside these ranges and needn't reach their ends.
There are 2 independent parts, one for each index of `groups`. The reference program is written for one: setup_inputs(seed, part) draws one part's arguments, and reference() takes and returns one part's arrays. A program takes and returns all parts, laid end to end along the dimension named above; an argument that names none is the same for every part. Nothing has to cross between parts.
Inputs may be any that keep to these rules, and one draw needn't show every extreme that they name: `reading_index`: row 0 is a reading's day, rows 1 to 3 the mesh nodes of its triangle's vertices. On every device, column block k (columns k * 64 to (k + 1) * 64 - 1) holds readings whose day lies in time partition k. `part_lengths`: partition k holds the days that follow those of partitions 0 to k - 1; exactly 8 partitions hold 2 days, the others 1. `reading_value`: row 0 is the linear predictor; rows 1 to 3 are positive barycentric weights summing to 1 for each reading. `spatial_prec`: A symmetric sparse mesh precision: each row has a few nonpositive neighbour entries, and a positive diagonal that exceeds the sum of magnitudes of its row's other entries.
All inputs are finite; a program needn't handle non-finite values.
Results may differ from the reference program's by a relative error of at most 0.0003.
Values sent between devices are 32-bit elements; how exact they have to be, the bound alone decides.
No kernel may reach another device: no remote copies, remote signals or barrier semaphores. Data moves between devices by JAX's collectives and lax.ppermute only.
A program may use at most 128 MiB of HBM per device.

```python
import jax
import jax.numpy as jnp
from jax import lax

M = 768
P_SIZE = 16
CAP = 64
READ_DEV = 1024
N_TM = 16


def partition_lengths(key):
    ranking = jax.random.permutation(jax.random.fold_in(key, 11), N_TM)
    return (1 + (ranking < N_TM // 2).astype(jnp.int32)).astype(jnp.int32)


def draw_part_lengths(key, part):
    return partition_lengths(key)


def draw_reading_index(key, part):
    lengths = partition_lengths(key)
    part_ends = (jnp.cumsum(lengths) - 1).astype(jnp.int32)
    bucket = jnp.arange(N_TM * CAP, dtype=jnp.int32) // CAP
    step_back = jax.random.randint(jax.random.fold_in(key, 12), (N_TM, N_TM * CAP), 0, 2).astype(jnp.int32)
    day_ids = part_ends[bucket][None, :] - step_back * (lengths[bucket][None, :] - 1)
    vertex_ids = jax.random.randint(jax.random.fold_in(key, 13), (3, N_TM, N_TM * CAP), 0, M).astype(jnp.int32)
    return jnp.concatenate([day_ids[None].astype(jnp.int32), vertex_ids], axis=0)


def draw_reading_value(key, part):
    first_key = jax.random.fold_in(key, 21)
    second_key = jax.random.fold_in(key, 22)
    linear = jnp.clip(0.5 * jax.random.normal(first_key, (N_TM, N_TM * CAP)), -1.5, 1.5)
    uniform_draws = jax.random.uniform(second_key, (3, N_TM, N_TM * CAP), minval=0.2, maxval=1.0)
    bary_weights = uniform_draws / jnp.sum(uniform_draws, axis=0, keepdims=True)
    return jnp.concatenate([linear[None], bary_weights], axis=0).astype(jnp.float32)


def draw_spatial_prec(key, part):
    offsets = [1, 2, 3, 5, 8, 13]
    rows = jnp.arange(M, dtype=jnp.int32)[:, None]
    cols = jnp.arange(M, dtype=jnp.int32)[None, :]
    distance = (cols - rows) % M
    magnitudes = jax.random.uniform(jax.random.fold_in(key, 31), (M, len(offsets)), minval=0.5, maxval=1.5)
    upper = jnp.zeros((M, M), jnp.float32)
    for index in range(len(offsets)):
        upper = upper + jnp.where(distance == offsets[index], magnitudes[:, index:index + 1], 0.0)
    neighbours = 0.125 * (upper + upper.T)
    row_total = jnp.sum(neighbours, axis=1)
    ratio = jax.random.uniform(jax.random.fold_in(key, 32), (M,), minval=0.5, maxval=0.9)
    identity = jnp.eye(M, dtype=jnp.float32)
    return (identity * (row_total / ratio)[None, :] - neighbours).astype(jnp.float32)


def block_scale(key, dims, split, least, high):
    loudness, own = 1.0, jax.random.fold_in(key, 6)
    for dim, parts in split:
        steps = jnp.exp(jax.random.uniform(jax.random.fold_in(own, dim), (parts,), jnp.float32, least / len(split), high / len(split)))
        loudness = loudness * jnp.repeat(steps, dims[dim] // parts).reshape([-1 if axis == dim else 1 for axis in range(len(dims))])
    return loudness


def scatter_about(key, extent, spread, reach, shards=(), kind=jnp.bfloat16):
    factor_of = block_scale(key, extent, shards, -0.22, 0.18) if shards else 1.0
    values = jax.random.normal(key, extent, jnp.float32) * spread * factor_of
    return jnp.minimum(jnp.maximum(values, -reach), reach).astype(kind)


def setup_inputs(seed: int = 0, part: int = 0) -> dict:
    key_of = jax.random.split(jax.random.key(seed), 7)
    part_splits = jax.random.split(jax.random.fold_in(key_of[6], part), 7)
    hyper = jnp.clip(jax.random.uniform(part_splits[0], (3,), jnp.float32, 0.5, 0.9), 0.5, 0.9)
    spatial_prec = draw_spatial_prec(jax.random.fold_in(key_of[6], 71), part)
    part_lengths = draw_part_lengths(jax.random.fold_in(jax.random.fold_in(key_of[6], part), 71), part)
    reading_index = draw_reading_index(jax.random.fold_in(jax.random.fold_in(key_of[6], part), 71), part)
    reading_value = draw_reading_value(jax.random.fold_in(jax.random.fold_in(key_of[6], part), 71), part)
    reading_cov = scatter_about(part_splits[5], (P_SIZE, N_TM, N_TM * CAP), READ_DEV ** -0.5, 0.1875, ((1, 16),), jnp.float32)
    return {"hyper": hyper, "spatial_prec": spatial_prec, "part_lengths": part_lengths, "reading_index": reading_index, "reading_value": reading_value, "reading_cov": reading_cov}


HIGHEST = lax.Precision.HIGHEST

def assemble(records_int, records_float, covariate, my_end, mesh_width):
    total_reads = records_int.shape[1] * records_int.shape[2]
    records_int = records_int.reshape(4, total_reads)
    records_float = records_float.reshape(4, total_reads)
    covariate = covariate.reshape(covariate.shape[0], total_reads)
    day_slot = (my_end - records_int[0]).astype(jnp.int32)
    weight = jnp.exp(records_float[0])
    vertex_ids = records_int[1:4]
    bary_weights = records_float[1:4]
    scaled = bary_weights * weight[None, :]
    block_start = day_slot * (mesh_width * mesh_width)
    positions = (block_start[None, None, :] + vertex_ids[:, None, :] * mesh_width + vertex_ids[None, :, :]).reshape(-1)
    entries = (scaled[:, None, :] * bary_weights[None, :, :]).reshape(-1)
    hessian = jnp.zeros((2 * mesh_width * mesh_width,), jnp.float32).at[positions].add(entries)
    hessian = hessian.reshape(2, mesh_width, mesh_width)
    border_rows = (day_slot[None, :] * mesh_width + vertex_ids).reshape(-1)
    border_terms = (covariate[:, None, :] * scaled[None, :, :]).reshape(covariate.shape[0], -1)
    border = jnp.zeros((covariate.shape[0], 2 * mesh_width), jnp.float32).at[:, border_rows].add(border_terms)
    border = border.reshape(covariate.shape[0], 2, mesh_width).transpose(1, 0, 2)
    tip_data = jnp.dot(covariate * weight[None, :], covariate.T, precision=HIGHEST)
    return (hessian, border, tip_data)

def eliminate(hessian, border, prior_diag, coupling_block):
    mesh_width = coupling_block.shape[0]
    interior = hessian[1] + prior_diag
    factor = jnp.linalg.cholesky(interior)
    stacked = jnp.concatenate([coupling_block, border[1].T], axis=1)
    solved = jax.scipy.linalg.solve_triangular(factor, stacked, lower=True)
    across = solved[:, :mesh_width]
    toward = solved[:, mesh_width:]
    schur_update = -jnp.dot(across.T, across, precision=HIGHEST)
    lateral_block = -jnp.dot(toward.T, across, precision=HIGHEST)
    apex_schur_block = -jnp.dot(toward.T, toward, precision=HIGHEST)
    return (schur_update, lateral_block, apex_schur_block)

def reference(hyper, spatial_prec, part_lengths, reading_index, reading_value, reading_cov):
    mesh_width = spatial_prec.shape[0]
    covars = reading_cov.shape[0]
    corr_time = hyper[0]
    tau_field = hyper[1]
    tau_fixed = hyper[2]
    prior_diag = (1.0 + corr_time * corr_time) * tau_field * spatial_prec
    coupling_block = -corr_time * tau_field * spatial_prec
    part_ends = (jnp.cumsum(part_lengths) - 1).astype(jnp.int32)

    def one_part(partition_position):
        start_col = (partition_position * CAP).astype(jnp.int32)
        records_int = lax.dynamic_slice_in_dim(reading_index, start_col, CAP, 2)
        records_float = lax.dynamic_slice_in_dim(reading_value, start_col, CAP, 2)
        covariate = lax.dynamic_slice_in_dim(reading_cov, start_col, CAP, 2)
        my_end = part_ends[partition_position]
        local_length = part_lengths[partition_position]
        hessian, border, tip_data = assemble(records_int, records_float, covariate, my_end, mesh_width)

        def perform_elimination():
            return eliminate(hessian, border, prior_diag, coupling_block)

        def bypass_elimination():
            return (jnp.zeros_like(coupling_block), jnp.zeros((covars, mesh_width), coupling_block.dtype), jnp.zeros((covars, covars), coupling_block.dtype))
        schur_update, lateral_block, apex_schur_block = lax.cond(local_length == 2, perform_elimination, bypass_elimination)
        has_left = partition_position > 0
        fill = jnp.where(has_left, jnp.where(local_length == 2, schur_update, coupling_block), 0.0)
        left_update = jnp.where(has_left, schur_update, 0.0)
        left_side = jnp.where(has_left, lateral_block, 0.0)
        own_sep = hessian[0] + prior_diag + schur_update
        own_border = border[0] + lateral_block
        return (own_sep, own_border, fill, left_update, left_side, tip_data + apex_schur_block)
    own_sep, own_border, fill, left_update, left_side, tip_parts = lax.map(one_part, jnp.arange(N_TM, dtype=jnp.int32))
    shifted_update = jnp.concatenate([left_update[1:], jnp.zeros_like(left_update[:1])], axis=0)
    shifted_side = jnp.concatenate([left_side[1:], jnp.zeros_like(left_side[:1])], axis=0)
    sep_block = own_sep + shifted_update
    sep_border = own_border + shifted_side
    tip = jnp.sum(tip_parts, axis=0) + tau_fixed * jnp.eye(covars, dtype=jnp.float32)
    return (sep_block, fill, sep_border, tip)
```

```python
import jax
import jax.numpy as jnp
from jax import lax
from jax.sharding import PartitionSpec as P

HIGHEST = lax.Precision.HIGHEST


def passed_along(x, axis, by):
    length = lax.axis_size(axis)
    pairs = [(i, i + by) for i in range(length) if 0 <= i + by < length]
    return lax.ppermute(x, axis, pairs)


def matmul_high(left, right):
    return jnp.dot(left, right, precision=HIGHEST)


def contract_rows(left, right):
    return lax.dot_general(left, right, (((0,), (0,)), ((), ())), precision=HIGHEST)


def assemble(packed, my_end, mesh_width, covars):
    total_reads = packed.shape[1] * packed.shape[2]
    packed = packed.reshape(packed.shape[0], total_reads)
    day = packed[0].astype(jnp.int32)
    vertex_ids = packed[1:4].astype(jnp.int32)
    weight = jnp.exp(packed[4])
    bary_weights = packed[5:8]
    covariate = packed[8 : 8 + covars]
    day_slot = my_end - day
    nodes = lax.broadcasted_iota(jnp.int32, (total_reads, mesh_width), 1)
    incidence = jnp.zeros((total_reads, mesh_width), jnp.float32)
    for u in range(3):
        incidence = incidence + jnp.where(
            vertex_ids[u][:, None] == nodes, bary_weights[u][:, None], 0.0
        )
    last_weight = jnp.where(day_slot == 0, weight, 0.0)
    inner_weight = jnp.where(day_slot == 1, weight, 0.0)
    weighted = jnp.concatenate(
        [incidence * last_weight[:, None], incidence * inner_weight[:, None]], axis=1
    )
    left = jnp.concatenate([incidence, covariate.T], axis=1)
    blocks = contract_rows(left, weighted)
    hessian = jnp.stack([blocks[:mesh_width, :mesh_width], blocks[:mesh_width, mesh_width:]])
    border = jnp.stack([blocks[mesh_width:, :mesh_width], blocks[mesh_width:, mesh_width:]])
    tip_data = jnp.dot(covariate * weight[None, :], covariate.T, precision=HIGHEST)
    return (hessian, border, tip_data)


def eliminate(hessian, border, prior_diag, coupling_block):
    mesh_width = coupling_block.shape[0]
    block_size = 128 if mesh_width % 128 == 0 else mesh_width
    count_blocks = mesh_width // block_size
    interior = hessian[1] + prior_diag
    work = jnp.concatenate([interior, coupling_block, border[1].T], axis=1)
    solved_rows = []
    for col in range(count_blocks):
        hi = (col + 1) * block_size
        factor = jnp.linalg.cholesky(work[:block_size, :block_size])
        solved = jax.scipy.linalg.solve_triangular(
            factor, work[:block_size, block_size:], lower=True
        )
        solved_rows.append(solved[:, mesh_width - hi :])
        if hi < mesh_width:
            below = solved[:, : mesh_width - hi]
            work = work[block_size:, block_size:] - contract_rows(below, solved)
    solved = jnp.concatenate(solved_rows, axis=0)
    across = solved[:, :mesh_width]
    toward = solved[:, mesh_width:]
    schur_update = -contract_rows(across, across)
    lateral_block = -contract_rows(toward, across)
    apex_schur_block = -contract_rows(toward, toward)
    return (schur_update, lateral_block, apex_schur_block)


def local(hyper, spatial_prec, part_lengths, reading_index, reading_value, reading_cov):
    packed = jnp.concatenate(
        [reading_index.astype(jnp.float32), reading_value, reading_cov], axis=0
    )
    packed = lax.all_to_all(packed, "tm", split_axis=2, concat_axis=1, tiled=True)
    mesh_width = spatial_prec.shape[0]
    covars = reading_cov.shape[0]
    partition_position = lax.axis_index("tm")
    corr_time = hyper[0]
    tau_field = hyper[1]
    tau_fixed = hyper[2]
    prior_diag = (1.0 + corr_time * corr_time) * tau_field * spatial_prec
    coupling_block = -corr_time * tau_field * spatial_prec
    part_ends = (jnp.cumsum(part_lengths) - 1).astype(jnp.int32)
    my_end = part_ends[partition_position]
    local_length = part_lengths[partition_position]
    hessian, border, tip_data = assemble(packed, my_end, mesh_width, covars)

    def bypass_elimination():
        return (
            jnp.zeros_like(coupling_block),
            jnp.zeros((covars, mesh_width), coupling_block.dtype),
            jnp.zeros((covars, covars), coupling_block.dtype),
        )

    def perform_elimination():
        return eliminate(hessian, border, prior_diag, coupling_block)

    schur_update, lateral_block, apex_schur_block = lax.cond(
        local_length == 2, perform_elimination, bypass_elimination
    )
    has_left = partition_position > 0
    fill = jnp.where(has_left, jnp.where(local_length == 2, schur_update, coupling_block), 0.0)
    left_update = jnp.where(has_left, schur_update, 0.0)
    left_side = jnp.where(has_left, lateral_block, 0.0)
    from_right, from_right_side = passed_along((left_update, left_side), "tm", -1)
    sep_block = hessian[0] + prior_diag + schur_update + from_right
    sep_border = border[0] + lateral_block + from_right_side
    tip_total = lax.psum(tip_data + apex_schur_block, "tm")
    tip = tip_total + tau_fixed * jnp.eye(covars, dtype=jnp.float32)
    return (sep_block[None], fill[None], sep_border[None], tip)


def solution(mesh):
    in_specs = (
        P("groups"),
        P(),
        P("groups"),
        P(None, ("groups", "tm"), None),
        P(None, ("groups", "tm"), None),
        P(None, ("groups", "tm"), None),
    )
    out_specs = (
        P(("groups", "tm"), None, None),
        P(("groups", "tm"), None, None),
        P(("groups", "tm"), None, None),
        P("groups", None),
    )
    return jax.shard_map(local, mesh=mesh, in_specs=in_specs, out_specs=out_specs, check_vma=False)
```

```python
import jax
import jax.numpy as jnp
from jax import lax
from jax.sharding import PartitionSpec as P
from jax.experimental import pallas as pl
from jax.experimental.pallas import tpu as pltpu

HIGHEST = lax.Precision.HIGHEST


def passed_along(x, axis, by):
    length = lax.axis_size(axis)
    pairs = [(i, i + by) for i in range(length) if 0 <= i + by < length]
    return lax.ppermute(x, axis, pairs)


def matmul_high(left, right):
    return jnp.dot(left, right, precision=HIGHEST)


def contract_rows(left, right):
    return lax.dot_general(left, right, (((0,), (0,)), ((), ())), precision=HIGHEST)


def split_dot(left, right):
    dims = (((1,), (1,)), ((), ()))
    left_hi = left.astype(jnp.bfloat16)
    left_lo = (left - left_hi.astype(jnp.float32)).astype(jnp.bfloat16)
    right_hi = right.astype(jnp.bfloat16)
    right_lo = (right - right_hi.astype(jnp.float32)).astype(jnp.bfloat16)
    out = lax.dot_general(left_hi, right_hi, dims, preferred_element_type=jnp.float32)
    out = out + lax.dot_general(left_hi, right_lo, dims, preferred_element_type=jnp.float32)
    out = out + lax.dot_general(left_lo, right_hi, dims, preferred_element_type=jnp.float32)
    return out


def assemble_kernel(end_ref, packed_ref, hessian_ref, border_ref, tip_ref):
    mesh_width = hessian_ref.shape[1]
    covars = border_ref.shape[1]

    @pl.when(pl.program_id(0) == 0)
    def _():
        hessian_ref[...] = jnp.zeros_like(hessian_ref)
        border_ref[...] = jnp.zeros_like(border_ref)
        tip_ref[...] = jnp.zeros_like(tip_ref)

    chunk = packed_ref.shape[1]
    my_end = end_ref[0]
    day = packed_ref[0:1, :]
    weight = jnp.exp(packed_ref[4:5, :])
    nodes = lax.broadcasted_iota(jnp.int32, (mesh_width, chunk), 0).astype(jnp.float32)
    incidence = jnp.zeros((mesh_width, chunk), jnp.float32)
    for u in range(3):
        incidence = incidence + jnp.where(
            nodes == packed_ref[1 + u : 2 + u, :], packed_ref[5 + u : 6 + u, :], 0.0
        )
    covariate = packed_ref[8 : 8 + covars, :]
    for slot in range(2):
        chosen = jnp.where(day == my_end - slot, weight, 0.0)
        weighted = incidence * chosen
        hessian_ref[slot] += split_dot(incidence, weighted)
        border_ref[slot] += split_dot(covariate, weighted)
    tip_ref[...] += split_dot(covariate * weight, covariate)


def assemble(packed, my_end, mesh_width, covars):
    total_reads = packed.shape[1] * packed.shape[2]
    rows = packed.shape[0]
    packed = packed.reshape(rows, total_reads)
    chunk = 512 if total_reads % 512 == 0 else total_reads
    end_value = my_end.astype(jnp.float32).reshape(1)
    hessian, border, tip_data = pl.pallas_call(
        assemble_kernel,
        grid=(total_reads // chunk,),
        in_specs=[
            pl.BlockSpec(memory_space=pltpu.SMEM),
            pl.BlockSpec((rows, chunk), lambda i: (0, i)),
        ],
        out_specs=[
            pl.BlockSpec((2, mesh_width, mesh_width), lambda i: (0, 0, 0)),
            pl.BlockSpec((2, covars, mesh_width), lambda i: (0, 0, 0)),
            pl.BlockSpec((covars, covars), lambda i: (0, 0)),
        ],
        out_shape=[
            jax.ShapeDtypeStruct((2, mesh_width, mesh_width), jnp.float32),
            jax.ShapeDtypeStruct((2, covars, mesh_width), jnp.float32),
            jax.ShapeDtypeStruct((covars, covars), jnp.float32),
        ],
        compiler_params=pltpu.CompilerParams(
            dimension_semantics=("arbitrary",), vmem_limit_bytes=48 * 1024 * 1024
        ),
    )(end_value, packed)
    return (hessian, border, tip_data)


def eliminate(hessian, border, prior_diag, coupling_block):
    mesh_width = coupling_block.shape[0]
    block_size = 128 if mesh_width % 128 == 0 else mesh_width
    count_blocks = mesh_width // block_size
    interior = hessian[1] + prior_diag
    work = jnp.concatenate([interior, coupling_block, border[1].T], axis=1)
    solved_rows = []
    for col in range(count_blocks):
        hi = (col + 1) * block_size
        factor = jnp.linalg.cholesky(work[:block_size, :block_size])
        solved = jax.scipy.linalg.solve_triangular(
            factor, work[:block_size, block_size:], lower=True
        )
        solved_rows.append(solved[:, mesh_width - hi :])
        if hi < mesh_width:
            below = solved[:, : mesh_width - hi]
            work = work[block_size:, block_size:] - contract_rows(below, solved)
    solved = jnp.concatenate(solved_rows, axis=0)
    across = solved[:, :mesh_width]
    toward = solved[:, mesh_width:]
    schur_update = -contract_rows(across, across)
    lateral_block = -contract_rows(toward, across)
    apex_schur_block = -contract_rows(toward, toward)
    return (schur_update, lateral_block, apex_schur_block)


def local(hyper, spatial_prec, part_lengths, reading_index, reading_value, reading_cov):
    packed = jnp.concatenate(
        [reading_index.astype(jnp.float32), reading_value, reading_cov], axis=0
    )
    packed = lax.all_to_all(packed, "tm", split_axis=2, concat_axis=1, tiled=True)
    mesh_width = spatial_prec.shape[0]
    covars = reading_cov.shape[0]
    partition_position = lax.axis_index("tm")
    corr_time = hyper[0]
    tau_field = hyper[1]
    tau_fixed = hyper[2]
    prior_diag = (1.0 + corr_time * corr_time) * tau_field * spatial_prec
    coupling_block = -corr_time * tau_field * spatial_prec
    part_ends = (jnp.cumsum(part_lengths) - 1).astype(jnp.int32)
    my_end = part_ends[partition_position]
    local_length = part_lengths[partition_position]
    hessian, border, tip_data = assemble(packed, my_end, mesh_width, covars)

    def bypass_elimination():
        return (
            jnp.zeros_like(coupling_block),
            jnp.zeros((covars, mesh_width), coupling_block.dtype),
            jnp.zeros((covars, covars), coupling_block.dtype),
        )

    def perform_elimination():
        return eliminate(hessian, border, prior_diag, coupling_block)

    schur_update, lateral_block, apex_schur_block = lax.cond(
        local_length == 2, perform_elimination, bypass_elimination
    )
    has_left = partition_position > 0
    fill = jnp.where(has_left, jnp.where(local_length == 2, schur_update, coupling_block), 0.0)
    left_update = jnp.where(has_left, schur_update, 0.0)
    left_side = jnp.where(has_left, lateral_block, 0.0)
    from_right, from_right_side = passed_along((left_update, left_side), "tm", -1)
    sep_block = hessian[0] + prior_diag + schur_update + from_right
    sep_border = border[0] + lateral_block + from_right_side
    tip_total = lax.psum(tip_data + apex_schur_block, "tm")
    tip = tip_total + tau_fixed * jnp.eye(covars, dtype=jnp.float32)
    return (sep_block[None], fill[None], sep_border[None], tip)


def solution(mesh):
    in_specs = (
        P("groups"),
        P(),
        P("groups"),
        P(None, ("groups", "tm"), None),
        P(None, ("groups", "tm"), None),
        P(None, ("groups", "tm"), None),
    )
    out_specs = (
        P(("groups", "tm"), None, None),
        P(("groups", "tm"), None, None),
        P(("groups", "tm"), None, None),
        P("groups", None),
    )
    return jax.shard_map(local, mesh=mesh, in_specs=in_specs, out_specs=out_specs, check_vma=False)
```

```python
import jax
import jax.numpy as jnp
from jax import lax
from jax.sharding import PartitionSpec as P
from jax.experimental import pallas as pl
from jax.experimental.pallas import tpu as pltpu

HIGHEST = lax.Precision.HIGHEST


def passed_along(x, axis, by):
    length = lax.axis_size(axis)
    pairs = [(i, i + by) for i in range(length) if 0 <= i + by < length]
    return lax.ppermute(x, axis, pairs)


def matmul_high(left, right):
    return jnp.dot(left, right, precision=HIGHEST)


def contract_rows(left, right):
    return lax.dot_general(left, right, (((0,), (0,)), ((), ())), precision=HIGHEST)


def split_dot(left, right):
    dims = (((1,), (1,)), ((), ()))
    left_hi = left.astype(jnp.bfloat16)
    left_lo = (left - left_hi.astype(jnp.float32)).astype(jnp.bfloat16)
    right_hi = right.astype(jnp.bfloat16)
    right_lo = (right - right_hi.astype(jnp.float32)).astype(jnp.bfloat16)
    out = lax.dot_general(left_hi, right_hi, dims, preferred_element_type=jnp.float32)
    out = out + lax.dot_general(left_hi, right_lo, dims, preferred_element_type=jnp.float32)
    out = out + lax.dot_general(left_lo, right_hi, dims, preferred_element_type=jnp.float32)
    return out


def assemble_kernel(end_ref, packed_ref, hessian_ref, border_ref, tip_ref):
    mesh_width = hessian_ref.shape[1]
    covars = border_ref.shape[1]

    @pl.when(pl.program_id(0) == 0)
    def _():
        hessian_ref[...] = jnp.zeros_like(hessian_ref)
        border_ref[...] = jnp.zeros_like(border_ref)
        tip_ref[...] = jnp.zeros_like(tip_ref)

    chunk = packed_ref.shape[1]
    my_end = end_ref[0]
    day = packed_ref[0:1, :]
    weight = jnp.exp(packed_ref[4:5, :])
    nodes = lax.broadcasted_iota(jnp.int32, (mesh_width, chunk), 0).astype(jnp.float32)
    incidence = jnp.zeros((mesh_width, chunk), jnp.float32)
    for u in range(3):
        incidence = incidence + jnp.where(
            nodes == packed_ref[1 + u : 2 + u, :], packed_ref[5 + u : 6 + u, :], 0.0
        )
    covariate = packed_ref[8 : 8 + covars, :]
    for slot in range(2):
        chosen = jnp.where(day == my_end - slot, weight, 0.0)
        weighted = incidence * chosen
        hessian_ref[slot] += split_dot(incidence, weighted)
        border_ref[slot] += split_dot(covariate, weighted)
    tip_ref[...] += split_dot(covariate * weight, covariate)


def assemble(packed, my_end, mesh_width, covars):
    total_reads = packed.shape[1] * packed.shape[2]
    rows = packed.shape[0]
    packed = packed.reshape(rows, total_reads)
    chunk = 512 if total_reads % 512 == 0 else total_reads
    end_value = my_end.astype(jnp.float32).reshape(1)
    hessian, border, tip_data = pl.pallas_call(
        assemble_kernel,
        grid=(total_reads // chunk,),
        in_specs=[
            pl.BlockSpec(memory_space=pltpu.SMEM),
            pl.BlockSpec((rows, chunk), lambda i: (0, i)),
        ],
        out_specs=[
            pl.BlockSpec((2, mesh_width, mesh_width), lambda i: (0, 0, 0)),
            pl.BlockSpec((2, covars, mesh_width), lambda i: (0, 0, 0)),
            pl.BlockSpec((covars, covars), lambda i: (0, 0)),
        ],
        out_shape=[
            jax.ShapeDtypeStruct((2, mesh_width, mesh_width), jnp.float32),
            jax.ShapeDtypeStruct((2, covars, mesh_width), jnp.float32),
            jax.ShapeDtypeStruct((covars, covars), jnp.float32),
        ],
        compiler_params=pltpu.CompilerParams(
            dimension_semantics=("arbitrary",), vmem_limit_bytes=48 * 1024 * 1024
        ),
    )(end_value, packed)
    return (hessian, border, tip_data)


def sweep_kernel(block_ref, out_ref):
    size = block_ref.shape[0]
    out_ref[...] = block_ref[...]
    lane = lax.broadcasted_iota(jnp.int32, (size, size), 1)
    sub = lax.broadcasted_iota(jnp.int32, (size, size), 0)
    lane_row = lax.broadcasted_iota(jnp.int32, (1, size), 1)

    def body(k, carry):
        current = out_ref[...]
        row = out_ref[pl.ds(k, 1), :]
        col = jnp.sum(jnp.where(lane == k, current, 0.0), axis=1, keepdims=True)
        pivot = jnp.sum(jnp.where(lane_row == k, row, 0.0), axis=1, keepdims=True)
        inverse = 1.0 / pivot
        scaled_row = row * inverse
        update = current - col * scaled_row
        update = jnp.where(sub == k, scaled_row, update)
        update = jnp.where(lane == k, col * inverse, update)
        update = jnp.where((sub == k) & (lane == k), -inverse, update)
        out_ref[...] = update
        return carry

    lax.fori_loop(0, size, body, 0)


def negated_inverse(block):
    return pl.pallas_call(
        sweep_kernel,
        out_shape=jax.ShapeDtypeStruct(block.shape, jnp.float32),
        in_specs=[pl.BlockSpec(memory_space=pltpu.VMEM)],
        out_specs=pl.BlockSpec(memory_space=pltpu.VMEM),
    )(block)


def eliminate(hessian, border, prior_diag, coupling_block):
    mesh_width = coupling_block.shape[0]
    block_size = 128 if mesh_width % 128 == 0 else mesh_width
    count_blocks = mesh_width // block_size
    interior = hessian[1] + prior_diag
    work = jnp.concatenate([interior, coupling_block, border[1].T], axis=1)
    rhs_rows = []
    solved_rows = []
    for col in range(count_blocks):
        lo = col * block_size
        hi = lo + block_size
        neg_inv = negated_inverse(work[:block_size, :block_size])
        solved = -matmul_high(neg_inv, work[:block_size, block_size:])
        rhs_rows.append(work[:block_size, mesh_width - lo :])
        solved_rows.append(solved[:, mesh_width - hi :])
        if hi < mesh_width:
            beside = work[:block_size, block_size : mesh_width - lo]
            work = work[block_size:, block_size:] - contract_rows(beside, solved)
    rhs = jnp.concatenate(rhs_rows, axis=0)
    solved = jnp.concatenate(solved_rows, axis=0)
    schur = -contract_rows(rhs, solved)
    schur_update = schur[:mesh_width, :mesh_width]
    lateral_block = schur[mesh_width:, :mesh_width]
    apex_schur_block = schur[mesh_width:, mesh_width:]
    return (schur_update, lateral_block, apex_schur_block)


def local(hyper, spatial_prec, part_lengths, reading_index, reading_value, reading_cov):
    packed = jnp.concatenate(
        [reading_index.astype(jnp.float32), reading_value, reading_cov], axis=0
    )
    packed = lax.all_to_all(packed, "tm", split_axis=2, concat_axis=1, tiled=True)
    mesh_width = spatial_prec.shape[0]
    covars = reading_cov.shape[0]
    partition_position = lax.axis_index("tm")
    corr_time = hyper[0]
    tau_field = hyper[1]
    tau_fixed = hyper[2]
    prior_diag = (1.0 + corr_time * corr_time) * tau_field * spatial_prec
    coupling_block = -corr_time * tau_field * spatial_prec
    part_ends = (jnp.cumsum(part_lengths) - 1).astype(jnp.int32)
    my_end = part_ends[partition_position]
    local_length = part_lengths[partition_position]
    hessian, border, tip_data = assemble(packed, my_end, mesh_width, covars)

    def bypass_elimination():
        return (
            jnp.zeros_like(coupling_block),
            jnp.zeros((covars, mesh_width), coupling_block.dtype),
            jnp.zeros((covars, covars), coupling_block.dtype),
        )

    def perform_elimination():
        return eliminate(hessian, border, prior_diag, coupling_block)

    schur_update, lateral_block, apex_schur_block = lax.cond(
        local_length == 2, perform_elimination, bypass_elimination
    )
    has_left = partition_position > 0
    fill = jnp.where(has_left, jnp.where(local_length == 2, schur_update, coupling_block), 0.0)
    left_update = jnp.where(has_left, schur_update, 0.0)
    left_side = jnp.where(has_left, lateral_block, 0.0)
    from_right, from_right_side = passed_along((left_update, left_side), "tm", -1)
    sep_block = hessian[0] + prior_diag + schur_update + from_right
    sep_border = border[0] + lateral_block + from_right_side
    tip_total = lax.psum(tip_data + apex_schur_block, "tm")
    tip = tip_total + tau_fixed * jnp.eye(covars, dtype=jnp.float32)
    return (sep_block[None], fill[None], sep_border[None], tip)


def solution(mesh):
    in_specs = (
        P("groups"),
        P(),
        P("groups"),
        P(None, ("groups", "tm"), None),
        P(None, ("groups", "tm"), None),
        P(None, ("groups", "tm"), None),
    )
    out_specs = (
        P(("groups", "tm"), None, None),
        P(("groups", "tm"), None, None),
        P(("groups", "tm"), None, None),
        P("groups", None),
    )
    return jax.shard_map(local, mesh=mesh, in_specs=in_specs, out_specs=out_specs, check_vma=False)
```

```python
import jax
import jax.numpy as jnp
from jax import lax
from jax.sharding import PartitionSpec as P
from jax.experimental import pallas as pl
from jax.experimental.pallas import tpu as pltpu

HIGHEST = lax.Precision.HIGHEST


def passed_along(x, axis, by):
    length = lax.axis_size(axis)
    pairs = [(i, i + by) for i in range(length) if 0 <= i + by < length]
    return lax.ppermute(x, axis, pairs)


def matmul_high(left, right):
    return jnp.dot(left, right, precision=HIGHEST)


def contract_rows(left, right):
    return lax.dot_general(
        left, right, (((0,), (0,)), ((), ())), preferred_element_type=jnp.float32
    )


def split_dot(left, right):
    dims = (((1,), (1,)), ((), ()))
    left_hi = left.astype(jnp.bfloat16)
    left_lo = (left - left_hi.astype(jnp.float32)).astype(jnp.bfloat16)
    right_hi = right.astype(jnp.bfloat16)
    right_lo = (right - right_hi.astype(jnp.float32)).astype(jnp.bfloat16)
    out = lax.dot_general(left_hi, right_hi, dims, preferred_element_type=jnp.float32)
    out = out + lax.dot_general(left_hi, right_lo, dims, preferred_element_type=jnp.float32)
    out = out + lax.dot_general(left_lo, right_hi, dims, preferred_element_type=jnp.float32)
    return out


def assemble_kernel(end_ref, packed_ref, hessian_ref, border_ref, tip_ref):
    mesh_width = hessian_ref.shape[1]
    covars = border_ref.shape[1]

    @pl.when(pl.program_id(0) == 0)
    def _():
        hessian_ref[...] = jnp.zeros_like(hessian_ref)
        border_ref[...] = jnp.zeros_like(border_ref)
        tip_ref[...] = jnp.zeros_like(tip_ref)

    chunk = packed_ref.shape[1]
    my_end = end_ref[0]
    day = packed_ref[0:1, :]
    weight = jnp.exp(packed_ref[4:5, :])
    nodes = lax.broadcasted_iota(jnp.int32, (mesh_width, chunk), 0).astype(jnp.float32)
    incidence = jnp.zeros((mesh_width, chunk), jnp.float32)
    for u in range(3):
        incidence = incidence + jnp.where(
            nodes == packed_ref[1 + u : 2 + u, :], packed_ref[5 + u : 6 + u, :], 0.0
        )
    covariate = packed_ref[8 : 8 + covars, :]
    for slot in range(2):
        chosen = jnp.where(day == my_end - slot, weight, 0.0)
        weighted = incidence * chosen
        hessian_ref[slot] += split_dot(incidence, weighted)
        border_ref[slot] += split_dot(covariate, weighted)
    tip_ref[...] += split_dot(covariate * weight, covariate)


def assemble(packed, my_end, mesh_width, covars):
    total_reads = packed.shape[1] * packed.shape[2]
    rows = packed.shape[0]
    packed = packed.reshape(rows, total_reads)
    chunk = 512 if total_reads % 512 == 0 else total_reads
    end_value = my_end.astype(jnp.float32).reshape(1)
    hessian, border, tip_data = pl.pallas_call(
        assemble_kernel,
        grid=(total_reads // chunk,),
        in_specs=[
            pl.BlockSpec(memory_space=pltpu.SMEM),
            pl.BlockSpec((rows, chunk), lambda i: (0, i)),
        ],
        out_specs=[
            pl.BlockSpec((2, mesh_width, mesh_width), lambda i: (0, 0, 0)),
            pl.BlockSpec((2, covars, mesh_width), lambda i: (0, 0, 0)),
            pl.BlockSpec((covars, covars), lambda i: (0, 0)),
        ],
        out_shape=[
            jax.ShapeDtypeStruct((2, mesh_width, mesh_width), jnp.float32),
            jax.ShapeDtypeStruct((2, covars, mesh_width), jnp.float32),
            jax.ShapeDtypeStruct((covars, covars), jnp.float32),
        ],
        compiler_params=pltpu.CompilerParams(
            dimension_semantics=("arbitrary",), vmem_limit_bytes=48 * 1024 * 1024
        ),
    )(end_value, packed)
    return (hessian, border, tip_data)


def split_parts(value):
    high = value.astype(jnp.bfloat16)
    low = (value - high.astype(jnp.float32)).astype(jnp.bfloat16)
    return high, low


def split_matmul(left, right):
    left_hi, left_lo = split_parts(left)
    right_hi, right_lo = split_parts(right)
    out = jnp.dot(left_hi, right_hi, preferred_element_type=jnp.float32)
    out = out + jnp.dot(left_hi, right_lo, preferred_element_type=jnp.float32)
    out = out + jnp.dot(left_lo, right_hi, preferred_element_type=jnp.float32)
    return out


def exact_matmul(left, right):
    return jnp.dot(left, right, precision=HIGHEST, preferred_element_type=jnp.float32)


def sweep(block_ref):
    size = block_ref.shape[0]
    lane = lax.broadcasted_iota(jnp.int32, (size, size), 1)
    sub = lax.broadcasted_iota(jnp.int32, (size, size), 0)
    lane_row = lax.broadcasted_iota(jnp.int32, (1, size), 1)

    def body(k, carry):
        current = block_ref[...]
        row = block_ref[pl.ds(k, 1), :]
        col = jnp.sum(jnp.where(lane == k, current, 0.0), axis=1, keepdims=True)
        pivot = jnp.sum(jnp.where(lane_row == k, row, 0.0), axis=1, keepdims=True)
        inverse = 1.0 / pivot
        scaled_row = row * inverse
        update = current - col * scaled_row
        update = jnp.where(sub == k, scaled_row, update)
        update = jnp.where(lane == k, col * inverse, update)
        update = jnp.where((sub == k) & (lane == k), -inverse, update)
        block_ref[...] = update
        return carry

    lax.fori_loop(0, size, body, 0)


def eliminate_kernel(start_ref, work_ref, solved_ref, block_ref):
    mesh_width = work_ref.shape[0]
    block_size = block_ref.shape[0]
    work_ref[...] = start_ref[...]
    for col in range(mesh_width // block_size):
        lo = col * block_size
        hi = lo + block_size
        block_ref[...] = work_ref[lo:hi, lo:hi]
        sweep(block_ref)
        solved = -exact_matmul(block_ref[...], work_ref[lo:hi, hi:])
        solved_ref[lo:hi, :] = solved[:, mesh_width - hi :]
        if hi < mesh_width:
            work_ref[hi:, hi:] = work_ref[hi:, hi:] - exact_matmul(work_ref[hi:, lo:hi], solved)


def eliminate(hessian, border, prior_diag, coupling_block):
    mesh_width = coupling_block.shape[0]
    block_size = 128 if mesh_width % 128 == 0 else mesh_width
    interior = hessian[1] + prior_diag
    start = jnp.concatenate([interior, coupling_block, border[1].T], axis=1)
    width = start.shape[1]
    work, solved = pl.pallas_call(
        eliminate_kernel,
        out_shape=[
            jax.ShapeDtypeStruct((mesh_width, width), jnp.float32),
            jax.ShapeDtypeStruct((mesh_width, width - mesh_width), jnp.float32),
        ],
        in_specs=[pl.BlockSpec(memory_space=pltpu.VMEM)],
        out_specs=[pl.BlockSpec(memory_space=pltpu.VMEM), pl.BlockSpec(memory_space=pltpu.VMEM)],
        scratch_shapes=[pltpu.VMEM((block_size, block_size), jnp.float32)],
        compiler_params=pltpu.CompilerParams(vmem_limit_bytes=60 * 1024 * 1024),
    )(start)
    schur = -lax.dot_general(
        work[:, mesh_width:], solved, (((0,), (0,)), ((), ())), precision=HIGHEST
    )
    schur_update = schur[:mesh_width, :mesh_width]
    lateral_block = schur[mesh_width:, :mesh_width]
    apex_schur_block = schur[mesh_width:, mesh_width:]
    return (schur_update, lateral_block, apex_schur_block)


def local(hyper, spatial_prec, part_lengths, reading_index, reading_value, reading_cov):
    packed = jnp.concatenate(
        [reading_index.astype(jnp.float32), reading_value, reading_cov], axis=0
    )
    packed = lax.all_to_all(packed, "tm", split_axis=2, concat_axis=1, tiled=True)
    mesh_width = spatial_prec.shape[0]
    covars = reading_cov.shape[0]
    partition_position = lax.axis_index("tm")
    corr_time = hyper[0]
    tau_field = hyper[1]
    tau_fixed = hyper[2]
    prior_diag = (1.0 + corr_time * corr_time) * tau_field * spatial_prec
    coupling_block = -corr_time * tau_field * spatial_prec
    part_ends = (jnp.cumsum(part_lengths) - 1).astype(jnp.int32)
    my_end = part_ends[partition_position]
    local_length = part_lengths[partition_position]
    hessian, border, tip_data = assemble(packed, my_end, mesh_width, covars)

    def bypass_elimination():
        return (
            jnp.zeros_like(coupling_block),
            jnp.zeros((covars, mesh_width), coupling_block.dtype),
            jnp.zeros((covars, covars), coupling_block.dtype),
        )

    def perform_elimination():
        return eliminate(hessian, border, prior_diag, coupling_block)

    schur_update, lateral_block, apex_schur_block = lax.cond(
        local_length == 2, perform_elimination, bypass_elimination
    )
    has_left = partition_position > 0
    fill = jnp.where(has_left, jnp.where(local_length == 2, schur_update, coupling_block), 0.0)
    left_update = jnp.where(has_left, schur_update, 0.0)
    left_side = jnp.where(has_left, lateral_block, 0.0)
    from_right, from_right_side = passed_along((left_update, left_side), "tm", -1)
    sep_block = hessian[0] + prior_diag + schur_update + from_right
    sep_border = border[0] + lateral_block + from_right_side
    tip_total = lax.psum(tip_data + apex_schur_block, "tm")
    tip = tip_total + tau_fixed * jnp.eye(covars, dtype=jnp.float32)
    return (sep_block[None], fill[None], sep_border[None], tip)


def solution(mesh):
    in_specs = (
        P("groups"),
        P(),
        P("groups"),
        P(None, ("groups", "tm"), None),
        P(None, ("groups", "tm"), None),
        P(None, ("groups", "tm"), None),
    )
    out_specs = (
        P(("groups", "tm"), None, None),
        P(("groups", "tm"), None, None),
        P(("groups", "tm"), None, None),
        P("groups", None),
    )
    return jax.shard_map(local, mesh=mesh, in_specs=in_specs, out_specs=out_specs, check_vma=False)
```

```python
import jax
import jax.numpy as jnp
from jax import lax
from jax.sharding import PartitionSpec as P
from jax.experimental import pallas as pl
from jax.experimental.pallas import tpu as pltpu

HIGHEST = lax.Precision.HIGHEST


def passed_along(x, axis, by):
    length = lax.axis_size(axis)
    pairs = [(i, i + by) for i in range(length) if 0 <= i + by < length]
    return lax.ppermute(x, axis, pairs)


def butterfly_sum(x, axis):
    length = lax.axis_size(axis)
    if length & (length - 1):
        return lax.psum(x, axis)
    stride = 1
    while stride < length:
        pairs = [(i, i ^ stride) for i in range(length)]
        x = x + lax.ppermute(x, axis, pairs)
        stride *= 2
    return x


def matmul_high(left, right):
    return jnp.dot(left, right, precision=HIGHEST)


def contract_rows(left, right):
    return lax.dot_general(
        left, right, (((0,), (0,)), ((), ())), preferred_element_type=jnp.float32
    )


def split_dot(left, right):
    dims = (((1,), (1,)), ((), ()))
    left_hi = left.astype(jnp.bfloat16)
    left_lo = (left - left_hi.astype(jnp.float32)).astype(jnp.bfloat16)
    right_hi = right.astype(jnp.bfloat16)
    right_lo = (right - right_hi.astype(jnp.float32)).astype(jnp.bfloat16)
    out = lax.dot_general(left_hi, right_hi, dims, preferred_element_type=jnp.float32)
    out = out + lax.dot_general(left_hi, right_lo, dims, preferred_element_type=jnp.float32)
    out = out + lax.dot_general(left_lo, right_hi, dims, preferred_element_type=jnp.float32)
    return out


def assemble_kernel(end_ref, packed_ref, hessian_ref, border_ref, tip_ref):
    mesh_width = hessian_ref.shape[1]
    covars = border_ref.shape[1]

    @pl.when(pl.program_id(0) == 0)
    def _():
        hessian_ref[...] = jnp.zeros_like(hessian_ref)
        border_ref[...] = jnp.zeros_like(border_ref)
        tip_ref[...] = jnp.zeros_like(tip_ref)

    chunk = packed_ref.shape[1]
    my_end = end_ref[0]
    day = packed_ref[0:1, :]
    weight = jnp.exp(packed_ref[4:5, :])
    nodes = lax.broadcasted_iota(jnp.int32, (mesh_width, chunk), 0).astype(jnp.float32)
    incidence = jnp.zeros((mesh_width, chunk), jnp.float32)
    for u in range(3):
        incidence = incidence + jnp.where(
            nodes == packed_ref[1 + u : 2 + u, :], packed_ref[5 + u : 6 + u, :], 0.0
        )
    covariate = packed_ref[8 : 8 + covars, :]
    for slot in range(2):
        chosen = jnp.where(day == my_end - slot, weight, 0.0)
        weighted = incidence * chosen
        hessian_ref[slot] += split_dot(incidence, weighted)
        border_ref[slot] += split_dot(covariate, weighted)
    tip_ref[...] += split_dot(covariate * weight, covariate)


def assemble(packed, my_end, mesh_width, covars):
    total_reads = packed.shape[1] * packed.shape[2]
    rows = packed.shape[0]
    packed = packed.reshape(rows, total_reads)
    chunk = 512 if total_reads % 512 == 0 else total_reads
    end_value = my_end.astype(jnp.float32).reshape(1)
    hessian, border, tip_data = pl.pallas_call(
        assemble_kernel,
        grid=(total_reads // chunk,),
        in_specs=[
            pl.BlockSpec(memory_space=pltpu.SMEM),
            pl.BlockSpec((rows, chunk), lambda i: (0, i)),
        ],
        out_specs=[
            pl.BlockSpec((2, mesh_width, mesh_width), lambda i: (0, 0, 0)),
            pl.BlockSpec((2, covars, mesh_width), lambda i: (0, 0, 0)),
            pl.BlockSpec((covars, covars), lambda i: (0, 0)),
        ],
        out_shape=[
            jax.ShapeDtypeStruct((2, mesh_width, mesh_width), jnp.float32),
            jax.ShapeDtypeStruct((2, covars, mesh_width), jnp.float32),
            jax.ShapeDtypeStruct((covars, covars), jnp.float32),
        ],
        compiler_params=pltpu.CompilerParams(
            dimension_semantics=("arbitrary",), vmem_limit_bytes=48 * 1024 * 1024
        ),
    )(end_value, packed)
    return (hessian, border, tip_data)


def split_parts(value):
    high = value.astype(jnp.bfloat16)
    low = (value - high.astype(jnp.float32)).astype(jnp.bfloat16)
    return high, low


def split_matmul(left, right):
    left_hi, left_lo = split_parts(left)
    right_hi, right_lo = split_parts(right)
    out = jnp.dot(left_hi, right_hi, preferred_element_type=jnp.float32)
    out = out + jnp.dot(left_hi, right_lo, preferred_element_type=jnp.float32)
    out = out + jnp.dot(left_lo, right_hi, preferred_element_type=jnp.float32)
    return out


def exact_matmul(left, right):
    return jnp.dot(left, right, precision=HIGHEST, preferred_element_type=jnp.float32)


def sweep(block_ref):
    size = block_ref.shape[0]
    lane = lax.broadcasted_iota(jnp.int32, (size, size), 1)
    sub = lax.broadcasted_iota(jnp.int32, (size, size), 0)
    lane_row = lax.broadcasted_iota(jnp.int32, (1, size), 1)

    def body(k, carry):
        current = block_ref[...]
        row = block_ref[pl.ds(k, 1), :]
        col = jnp.sum(jnp.where(lane == k, current, 0.0), axis=1, keepdims=True)
        pivot = jnp.sum(jnp.where(lane_row == k, row, 0.0), axis=1, keepdims=True)
        inverse = 1.0 / pivot
        scaled_row = row * inverse
        update = current - col * scaled_row
        update = jnp.where(sub == k, scaled_row, update)
        update = jnp.where(lane == k, col * inverse, update)
        update = jnp.where((sub == k) & (lane == k), -inverse, update)
        block_ref[...] = update
        return carry

    lax.fori_loop(0, size, body, 0)


def eliminate_kernel(start_ref, work_ref, solved_ref, block_ref):
    mesh_width = work_ref.shape[0]
    block_size = block_ref.shape[0]
    work_ref[...] = start_ref[...]
    for col in range(mesh_width // block_size):
        lo = col * block_size
        hi = lo + block_size
        block_ref[...] = work_ref[lo:hi, lo:hi]
        sweep(block_ref)
        solved = -exact_matmul(block_ref[...], work_ref[lo:hi, hi:])
        solved_ref[lo:hi, :] = solved[:, mesh_width - hi :]
        if hi < mesh_width:
            work_ref[hi:, hi:] = work_ref[hi:, hi:] - exact_matmul(work_ref[hi:, lo:hi], solved)


def eliminate(hessian, border, prior_diag, coupling_block):
    mesh_width = coupling_block.shape[0]
    block_size = 128 if mesh_width % 128 == 0 else mesh_width
    interior = hessian[1] + prior_diag
    start = jnp.concatenate([interior, coupling_block, border[1].T], axis=1)
    width = start.shape[1]
    work, solved = pl.pallas_call(
        eliminate_kernel,
        out_shape=[
            jax.ShapeDtypeStruct((mesh_width, width), jnp.float32),
            jax.ShapeDtypeStruct((mesh_width, width - mesh_width), jnp.float32),
        ],
        in_specs=[pl.BlockSpec(memory_space=pltpu.VMEM)],
        out_specs=[pl.BlockSpec(memory_space=pltpu.VMEM), pl.BlockSpec(memory_space=pltpu.VMEM)],
        scratch_shapes=[pltpu.VMEM((block_size, block_size), jnp.float32)],
        compiler_params=pltpu.CompilerParams(vmem_limit_bytes=60 * 1024 * 1024),
    )(start)
    schur = -lax.dot_general(
        work[:, mesh_width:], solved, (((0,), (0,)), ((), ())), precision=HIGHEST
    )
    schur_update = schur[:mesh_width, :mesh_width]
    lateral_block = schur[mesh_width:, :mesh_width]
    apex_schur_block = schur[mesh_width:, mesh_width:]
    return (schur_update, lateral_block, apex_schur_block)


def local(hyper, spatial_prec, part_lengths, reading_index, reading_value, reading_cov):
    packed = jnp.concatenate(
        [reading_index.astype(jnp.float32), reading_value, reading_cov], axis=0
    )
    packed = lax.all_to_all(packed, "tm", split_axis=2, concat_axis=1, tiled=True)
    mesh_width = spatial_prec.shape[0]
    covars = reading_cov.shape[0]
    partition_position = lax.axis_index("tm")
    corr_time = hyper[0]
    tau_field = hyper[1]
    tau_fixed = hyper[2]
    prior_diag = (1.0 + corr_time * corr_time) * tau_field * spatial_prec
    coupling_block = -corr_time * tau_field * spatial_prec
    part_ends = (jnp.cumsum(part_lengths) - 1).astype(jnp.int32)
    my_end = part_ends[partition_position]
    local_length = part_lengths[partition_position]
    hessian, border, tip_data = assemble(packed, my_end, mesh_width, covars)

    def bypass_elimination():
        return (
            jnp.zeros_like(coupling_block),
            jnp.zeros((covars, mesh_width), coupling_block.dtype),
            jnp.zeros((covars, covars), coupling_block.dtype),
        )

    def perform_elimination():
        return eliminate(hessian, border, prior_diag, coupling_block)

    schur_update, lateral_block, apex_schur_block = lax.cond(
        local_length == 2, perform_elimination, bypass_elimination
    )
    has_left = partition_position > 0
    fill = jnp.where(has_left, jnp.where(local_length == 2, schur_update, coupling_block), 0.0)
    left_update = jnp.where(has_left, schur_update, 0.0)
    left_side = jnp.where(has_left, lateral_block, 0.0)
    from_right, from_right_side = passed_along((left_update, left_side), "tm", -1)
    sep_block = hessian[0] + prior_diag + schur_update + from_right
    sep_border = border[0] + lateral_block + from_right_side
    tip_total = butterfly_sum(tip_data + apex_schur_block, "tm")
    tip = tip_total + tau_fixed * jnp.eye(covars, dtype=jnp.float32)
    return (sep_block[None], fill[None], sep_border[None], tip)


def solution(mesh):
    in_specs = (
        P("groups"),
        P(),
        P("groups"),
        P(None, ("groups", "tm"), None),
        P(None, ("groups", "tm"), None),
        P(None, ("groups", "tm"), None),
    )
    out_specs = (
        P(("groups", "tm"), None, None),
        P(("groups", "tm"), None, None),
        P(("groups", "tm"), None, None),
        P("groups", None),
    )
    return jax.shard_map(local, mesh=mesh, in_specs=in_specs, out_specs=out_specs, check_vma=False)
```

```python
import jax
import jax.numpy as jnp
from jax import lax
from jax.sharding import PartitionSpec as P
from jax.experimental import pallas as pl
from jax.experimental.pallas import tpu as pltpu

HIGHEST = lax.Precision.HIGHEST


def passed_along(x, axis, by):
    length = lax.axis_size(axis)
    pairs = [(i, i + by) for i in range(length) if 0 <= i + by < length]
    return lax.ppermute(x, axis, pairs)


def butterfly_sum(x, axis):
    length = lax.axis_size(axis)
    if length & (length - 1):
        return lax.psum(x, axis)
    stride = 1
    while stride < length:
        pairs = [(i, i ^ stride) for i in range(length)]
        x = x + lax.ppermute(x, axis, pairs)
        stride *= 2
    return x


def matmul_high(left, right):
    return jnp.dot(left, right, precision=HIGHEST)


def contract_rows(left, right):
    return lax.dot_general(
        left, right, (((0,), (0,)), ((), ())), preferred_element_type=jnp.float32
    )


def split_dot(left, right):
    dims = (((1,), (1,)), ((), ()))
    left_hi = left.astype(jnp.bfloat16)
    left_lo = (left - left_hi.astype(jnp.float32)).astype(jnp.bfloat16)
    right_hi = right.astype(jnp.bfloat16)
    right_lo = (right - right_hi.astype(jnp.float32)).astype(jnp.bfloat16)
    out = lax.dot_general(left_hi, right_hi, dims, preferred_element_type=jnp.float32)
    out = out + lax.dot_general(left_hi, right_lo, dims, preferred_element_type=jnp.float32)
    out = out + lax.dot_general(left_lo, right_hi, dims, preferred_element_type=jnp.float32)
    return out


def assemble_kernel(end_ref, packed_ref, hessian_ref, border_ref, tip_ref):
    mesh_width = hessian_ref.shape[1]
    covars = border_ref.shape[1]

    @pl.when(pl.program_id(0) == 0)
    def _():
        hessian_ref[...] = jnp.zeros_like(hessian_ref)
        border_ref[...] = jnp.zeros_like(border_ref)
        tip_ref[...] = jnp.zeros_like(tip_ref)

    chunk = packed_ref.shape[1]
    my_end = end_ref[0]
    day = packed_ref[0:1, :]
    weight = jnp.exp(packed_ref[4:5, :])
    nodes = lax.broadcasted_iota(jnp.int32, (mesh_width, chunk), 0).astype(jnp.float32)
    incidence = jnp.zeros((mesh_width, chunk), jnp.float32)
    for u in range(3):
        incidence = incidence + jnp.where(
            nodes == packed_ref[1 + u : 2 + u, :], packed_ref[5 + u : 6 + u, :], 0.0
        )
    covariate = packed_ref[8 : 8 + covars, :]
    for slot in range(2):
        chosen = jnp.where(day == my_end - slot, weight, 0.0)
        weighted = incidence * chosen
        hessian_ref[slot] += split_dot(incidence, weighted)
        border_ref[slot] += split_dot(covariate, weighted)
    tip_ref[...] += split_dot(covariate * weight, covariate)


def assemble(packed, my_end, mesh_width, covars):
    total_reads = packed.shape[1] * packed.shape[2]
    rows = packed.shape[0]
    packed = packed.reshape(rows, total_reads)
    chunk = 512 if total_reads % 512 == 0 else total_reads
    end_value = my_end.astype(jnp.float32).reshape(1)
    hessian, border, tip_data = pl.pallas_call(
        assemble_kernel,
        grid=(total_reads // chunk,),
        in_specs=[
            pl.BlockSpec(memory_space=pltpu.SMEM),
            pl.BlockSpec((rows, chunk), lambda i: (0, i)),
        ],
        out_specs=[
            pl.BlockSpec((2, mesh_width, mesh_width), lambda i: (0, 0, 0)),
            pl.BlockSpec((2, covars, mesh_width), lambda i: (0, 0, 0)),
            pl.BlockSpec((covars, covars), lambda i: (0, 0)),
        ],
        out_shape=[
            jax.ShapeDtypeStruct((2, mesh_width, mesh_width), jnp.float32),
            jax.ShapeDtypeStruct((2, covars, mesh_width), jnp.float32),
            jax.ShapeDtypeStruct((covars, covars), jnp.float32),
        ],
        compiler_params=pltpu.CompilerParams(
            dimension_semantics=("arbitrary",), vmem_limit_bytes=48 * 1024 * 1024
        ),
    )(end_value, packed)
    return (hessian, border, tip_data)


def split_parts(value):
    high = value.astype(jnp.bfloat16)
    low = (value - high.astype(jnp.float32)).astype(jnp.bfloat16)
    return high, low


def split_matmul(left, right):
    left_hi, left_lo = split_parts(left)
    right_hi, right_lo = split_parts(right)
    out = jnp.dot(left_hi, right_hi, preferred_element_type=jnp.float32)
    out = out + jnp.dot(left_hi, right_lo, preferred_element_type=jnp.float32)
    out = out + jnp.dot(left_lo, right_hi, preferred_element_type=jnp.float32)
    return out


def exact_matmul(left, right):
    return jnp.dot(left, right, precision=HIGHEST, preferred_element_type=jnp.float32)


def sweep(block_ref):
    size = block_ref.shape[0]
    lane = lax.broadcasted_iota(jnp.int32, (size, size), 1)
    sub = lax.broadcasted_iota(jnp.int32, (size, size), 0)
    lane_row = lax.broadcasted_iota(jnp.int32, (1, size), 1)

    def body(k, carry):
        current = block_ref[...]
        row = block_ref[pl.ds(k, 1), :]
        col = jnp.sum(jnp.where(lane == k, current, 0.0), axis=1, keepdims=True)
        pivot = jnp.sum(jnp.where(lane_row == k, row, 0.0), axis=1, keepdims=True)
        inverse = 1.0 / pivot
        scaled_row = row * inverse
        update = current - col * scaled_row
        update = jnp.where(sub == k, scaled_row, update)
        update = jnp.where(lane == k, col * inverse, update)
        update = jnp.where((sub == k) & (lane == k), -inverse, update)
        block_ref[...] = update
        return carry

    lax.fori_loop(0, size, body, 0, unroll=4)


def eliminate_kernel(start_ref, work_ref, solved_ref, block_ref):
    mesh_width = work_ref.shape[0]
    block_size = block_ref.shape[0]
    work_ref[...] = start_ref[...]
    for col in range(mesh_width // block_size):
        lo = col * block_size
        hi = lo + block_size
        block_ref[...] = work_ref[lo:hi, lo:hi]
        sweep(block_ref)
        solved = -exact_matmul(block_ref[...], work_ref[lo:hi, hi:])
        solved_ref[lo:hi, :] = solved[:, mesh_width - hi :]
        if hi < mesh_width:
            work_ref[hi:, hi:] = work_ref[hi:, hi:] - exact_matmul(work_ref[hi:, lo:hi], solved)


def eliminate(hessian, border, prior_diag, coupling_block):
    mesh_width = coupling_block.shape[0]
    block_size = 128 if mesh_width % 128 == 0 else mesh_width
    interior = hessian[1] + prior_diag
    start = jnp.concatenate([interior, coupling_block, border[1].T], axis=1)
    width = start.shape[1]
    work, solved = pl.pallas_call(
        eliminate_kernel,
        out_shape=[
            jax.ShapeDtypeStruct((mesh_width, width), jnp.float32),
            jax.ShapeDtypeStruct((mesh_width, width - mesh_width), jnp.float32),
        ],
        in_specs=[pl.BlockSpec(memory_space=pltpu.VMEM)],
        out_specs=[pl.BlockSpec(memory_space=pltpu.VMEM), pl.BlockSpec(memory_space=pltpu.VMEM)],
        scratch_shapes=[pltpu.VMEM((block_size, block_size), jnp.float32)],
        compiler_params=pltpu.CompilerParams(vmem_limit_bytes=60 * 1024 * 1024),
    )(start)
    schur = -lax.dot_general(
        work[:, mesh_width:], solved, (((0,), (0,)), ((), ())), precision=HIGHEST
    )
    schur_update = schur[:mesh_width, :mesh_width]
    lateral_block = schur[mesh_width:, :mesh_width]
    apex_schur_block = schur[mesh_width:, mesh_width:]
    return (schur_update, lateral_block, apex_schur_block)


def local(hyper, spatial_prec, part_lengths, reading_index, reading_value, reading_cov):
    packed = jnp.concatenate(
        [reading_index.astype(jnp.float32), reading_value, reading_cov], axis=0
    )
    packed = lax.all_to_all(packed, "tm", split_axis=2, concat_axis=1, tiled=True)
    mesh_width = spatial_prec.shape[0]
    covars = reading_cov.shape[0]
    partition_position = lax.axis_index("tm")
    corr_time = hyper[0]
    tau_field = hyper[1]
    tau_fixed = hyper[2]
    prior_diag = (1.0 + corr_time * corr_time) * tau_field * spatial_prec
    coupling_block = -corr_time * tau_field * spatial_prec
    part_ends = (jnp.cumsum(part_lengths) - 1).astype(jnp.int32)
    my_end = part_ends[partition_position]
    local_length = part_lengths[partition_position]
    hessian, border, tip_data = assemble(packed, my_end, mesh_width, covars)

    def bypass_elimination():
        return (
            jnp.zeros_like(coupling_block),
            jnp.zeros((covars, mesh_width), coupling_block.dtype),
            jnp.zeros((covars, covars), coupling_block.dtype),
        )

    def perform_elimination():
        return eliminate(hessian, border, prior_diag, coupling_block)

    schur_update, lateral_block, apex_schur_block = lax.cond(
        local_length == 2, perform_elimination, bypass_elimination
    )
    has_left = partition_position > 0
    fill = jnp.where(has_left, jnp.where(local_length == 2, schur_update, coupling_block), 0.0)
    left_update = jnp.where(has_left, schur_update, 0.0)
    left_side = jnp.where(has_left, lateral_block, 0.0)
    from_right, from_right_side = passed_along((left_update, left_side), "tm", -1)
    sep_block = hessian[0] + prior_diag + schur_update + from_right
    sep_border = border[0] + lateral_block + from_right_side
    tip_total = butterfly_sum(tip_data + apex_schur_block, "tm")
    tip = tip_total + tau_fixed * jnp.eye(covars, dtype=jnp.float32)
    return (sep_block[None], fill[None], sep_border[None], tip)


def solution(mesh):
    in_specs = (
        P("groups"),
        P(),
        P("groups"),
        P(None, ("groups", "tm"), None),
        P(None, ("groups", "tm"), None),
        P(None, ("groups", "tm"), None),
    )
    out_specs = (
        P(("groups", "tm"), None, None),
        P(("groups", "tm"), None, None),
        P(("groups", "tm"), None, None),
        P("groups", None),
    )
    return jax.shard_map(local, mesh=mesh, in_specs=in_specs, out_specs=out_specs, check_vma=False)
```

```python
import jax
import jax.numpy as jnp
from jax import lax
from jax.sharding import PartitionSpec as P
from jax.experimental import pallas as pl
from jax.experimental.pallas import tpu as pltpu

HIGHEST = lax.Precision.HIGHEST


def passed_along(x, axis, by):
    length = lax.axis_size(axis)
    pairs = [(i, i + by) for i in range(length) if 0 <= i + by < length]
    return lax.ppermute(x, axis, pairs)


def butterfly_sum(x, axis):
    length = lax.axis_size(axis)
    if length & (length - 1):
        return lax.psum(x, axis)
    stride = 1
    while stride < length:
        pairs = [(i, i ^ stride) for i in range(length)]
        x = x + lax.ppermute(x, axis, pairs)
        stride *= 2
    return x


def block_grid(mesh_width):
    size = 128 if mesh_width % 128 == 0 else mesh_width
    return size, mesh_width // size


def lower_blocks(matrix):
    size, count = block_grid(matrix.shape[0])
    tiles = [
        matrix[i * size : (i + 1) * size, j * size : (j + 1) * size]
        for i in range(count)
        for j in range(i + 1)
    ]
    return jnp.stack(tiles)


def from_lower_blocks(packed, mesh_width):
    size, count = block_grid(mesh_width)
    index = {}
    for i in range(count):
        for j in range(i + 1):
            index[i, j] = len(index)
    rows = []
    for i in range(count):
        row = [packed[index[i, j]] if j <= i else packed[index[j, i]].T for j in range(count)]
        rows.append(jnp.concatenate(row, axis=1))
    return jnp.concatenate(rows, axis=0)


def matmul_high(left, right):
    return jnp.dot(left, right, precision=HIGHEST)


def contract_rows(left, right):
    return lax.dot_general(
        left, right, (((0,), (0,)), ((), ())), preferred_element_type=jnp.float32
    )


def split_dot(left, right):
    dims = (((1,), (1,)), ((), ()))
    left_hi = left.astype(jnp.bfloat16)
    left_lo = (left - left_hi.astype(jnp.float32)).astype(jnp.bfloat16)
    right_hi = right.astype(jnp.bfloat16)
    right_lo = (right - right_hi.astype(jnp.float32)).astype(jnp.bfloat16)
    out = lax.dot_general(left_hi, right_hi, dims, preferred_element_type=jnp.float32)
    out = out + lax.dot_general(left_hi, right_lo, dims, preferred_element_type=jnp.float32)
    out = out + lax.dot_general(left_lo, right_hi, dims, preferred_element_type=jnp.float32)
    return out


def assemble_kernel(end_ref, packed_ref, hessian_ref, border_ref, tip_ref):
    mesh_width = hessian_ref.shape[1]
    covars = border_ref.shape[1]

    @pl.when(pl.program_id(0) == 0)
    def _():
        hessian_ref[...] = jnp.zeros_like(hessian_ref)
        border_ref[...] = jnp.zeros_like(border_ref)
        tip_ref[...] = jnp.zeros_like(tip_ref)

    chunk = packed_ref.shape[1]
    my_end = end_ref[0]
    day = packed_ref[0:1, :]
    weight = jnp.exp(packed_ref[4:5, :])
    nodes = lax.broadcasted_iota(jnp.int32, (mesh_width, chunk), 0).astype(jnp.float32)
    incidence = jnp.zeros((mesh_width, chunk), jnp.float32)
    for u in range(3):
        incidence = incidence + jnp.where(
            nodes == packed_ref[1 + u : 2 + u, :], packed_ref[5 + u : 6 + u, :], 0.0
        )
    covariate = packed_ref[8 : 8 + covars, :]
    for slot in range(2):
        chosen = jnp.where(day == my_end - slot, weight, 0.0)
        weighted = incidence * chosen
        hessian_ref[slot] += split_dot(incidence, weighted)
        border_ref[slot] += split_dot(covariate, weighted)
    tip_ref[...] += split_dot(covariate * weight, covariate)


def assemble(packed, my_end, mesh_width, covars):
    total_reads = packed.shape[1] * packed.shape[2]
    rows = packed.shape[0]
    packed = packed.reshape(rows, total_reads)
    chunk = 512 if total_reads % 512 == 0 else total_reads
    end_value = my_end.astype(jnp.float32).reshape(1)
    hessian, border, tip_data = pl.pallas_call(
        assemble_kernel,
        grid=(total_reads // chunk,),
        in_specs=[
            pl.BlockSpec(memory_space=pltpu.SMEM),
            pl.BlockSpec((rows, chunk), lambda i: (0, i)),
        ],
        out_specs=[
            pl.BlockSpec((2, mesh_width, mesh_width), lambda i: (0, 0, 0)),
            pl.BlockSpec((2, covars, mesh_width), lambda i: (0, 0, 0)),
            pl.BlockSpec((covars, covars), lambda i: (0, 0)),
        ],
        out_shape=[
            jax.ShapeDtypeStruct((2, mesh_width, mesh_width), jnp.float32),
            jax.ShapeDtypeStruct((2, covars, mesh_width), jnp.float32),
            jax.ShapeDtypeStruct((covars, covars), jnp.float32),
        ],
        compiler_params=pltpu.CompilerParams(
            dimension_semantics=("arbitrary",), vmem_limit_bytes=48 * 1024 * 1024
        ),
    )(end_value, packed)
    return (hessian, border, tip_data)


def split_parts(value):
    high = value.astype(jnp.bfloat16)
    low = (value - high.astype(jnp.float32)).astype(jnp.bfloat16)
    return high, low


def split_matmul(left, right):
    left_hi, left_lo = split_parts(left)
    right_hi, right_lo = split_parts(right)
    out = jnp.dot(left_hi, right_hi, preferred_element_type=jnp.float32)
    out = out + jnp.dot(left_hi, right_lo, preferred_element_type=jnp.float32)
    out = out + jnp.dot(left_lo, right_hi, preferred_element_type=jnp.float32)
    return out


def exact_matmul(left, right):
    return jnp.dot(left, right, precision=HIGHEST, preferred_element_type=jnp.float32)


def sweep(block_ref):
    size = block_ref.shape[0]
    lane = lax.broadcasted_iota(jnp.int32, (size, size), 1)
    sub = lax.broadcasted_iota(jnp.int32, (size, size), 0)
    lane_row = lax.broadcasted_iota(jnp.int32, (1, size), 1)

    def body(k, carry):
        current = block_ref[...]
        row = block_ref[pl.ds(k, 1), :]
        col = jnp.sum(jnp.where(lane == k, current, 0.0), axis=1, keepdims=True)
        pivot = jnp.sum(jnp.where(lane_row == k, row, 0.0), axis=1, keepdims=True)
        inverse = 1.0 / pivot
        scaled_row = row * inverse
        update = current - col * scaled_row
        update = jnp.where(sub == k, scaled_row, update)
        update = jnp.where(lane == k, col * inverse, update)
        update = jnp.where((sub == k) & (lane == k), -inverse, update)
        block_ref[...] = update
        return carry

    lax.fori_loop(0, size, body, 0)


def eliminate_kernel(start_ref, work_ref, solved_ref, block_ref):
    mesh_width = work_ref.shape[0]
    block_size = block_ref.shape[0]
    work_ref[...] = start_ref[...]
    for col in range(mesh_width // block_size):
        lo = col * block_size
        hi = lo + block_size
        block_ref[...] = work_ref[lo:hi, lo:hi]
        sweep(block_ref)
        solved = -exact_matmul(block_ref[...], work_ref[lo:hi, hi:])
        solved_ref[lo:hi, :] = solved[:, mesh_width - hi :]
        if hi < mesh_width:
            work_ref[hi:, hi:] = work_ref[hi:, hi:] - exact_matmul(work_ref[hi:, lo:hi], solved)


def eliminate(hessian, border, prior_diag, coupling_block):
    mesh_width = coupling_block.shape[0]
    block_size = 128 if mesh_width % 128 == 0 else mesh_width
    interior = hessian[1] + prior_diag
    start = jnp.concatenate([interior, coupling_block, border[1].T], axis=1)
    width = start.shape[1]
    work, solved = pl.pallas_call(
        eliminate_kernel,
        out_shape=[
            jax.ShapeDtypeStruct((mesh_width, width), jnp.float32),
            jax.ShapeDtypeStruct((mesh_width, width - mesh_width), jnp.float32),
        ],
        in_specs=[pl.BlockSpec(memory_space=pltpu.VMEM)],
        out_specs=[pl.BlockSpec(memory_space=pltpu.VMEM), pl.BlockSpec(memory_space=pltpu.VMEM)],
        scratch_shapes=[pltpu.VMEM((block_size, block_size), jnp.float32)],
        compiler_params=pltpu.CompilerParams(vmem_limit_bytes=60 * 1024 * 1024),
    )(start)
    schur = -lax.dot_general(
        work[:, mesh_width:], solved, (((0,), (0,)), ((), ())), precision=HIGHEST
    )
    schur_update = schur[:mesh_width, :mesh_width]
    lateral_block = schur[mesh_width:, :mesh_width]
    apex_schur_block = schur[mesh_width:, mesh_width:]
    return (schur_update, lateral_block, apex_schur_block)


def local(hyper, spatial_prec, part_lengths, reading_index, reading_value, reading_cov):
    packed = jnp.concatenate(
        [reading_index.astype(jnp.float32), reading_value, reading_cov], axis=0
    )
    packed = lax.all_to_all(packed, "tm", split_axis=2, concat_axis=1, tiled=True)
    mesh_width = spatial_prec.shape[0]
    covars = reading_cov.shape[0]
    partition_position = lax.axis_index("tm")
    corr_time = hyper[0]
    tau_field = hyper[1]
    tau_fixed = hyper[2]
    prior_diag = (1.0 + corr_time * corr_time) * tau_field * spatial_prec
    coupling_block = -corr_time * tau_field * spatial_prec
    part_ends = (jnp.cumsum(part_lengths) - 1).astype(jnp.int32)
    my_end = part_ends[partition_position]
    local_length = part_lengths[partition_position]
    hessian, border, tip_data = assemble(packed, my_end, mesh_width, covars)

    def bypass_elimination():
        return (
            jnp.zeros_like(coupling_block),
            jnp.zeros((covars, mesh_width), coupling_block.dtype),
            jnp.zeros((covars, covars), coupling_block.dtype),
        )

    def perform_elimination():
        return eliminate(hessian, border, prior_diag, coupling_block)

    schur_update, lateral_block, apex_schur_block = lax.cond(
        local_length == 2, perform_elimination, bypass_elimination
    )
    has_left = partition_position > 0
    fill = jnp.where(has_left, jnp.where(local_length == 2, schur_update, coupling_block), 0.0)
    left_update = jnp.where(has_left, schur_update, 0.0)
    left_side = jnp.where(has_left, lateral_block, 0.0)
    packed_update = lower_blocks(left_update)
    packed_update, from_right_side = passed_along((packed_update, left_side), "tm", -1)
    from_right = from_lower_blocks(packed_update, mesh_width)
    sep_block = hessian[0] + prior_diag + schur_update + from_right
    sep_border = border[0] + lateral_block + from_right_side
    tip_total = butterfly_sum(tip_data + apex_schur_block, "tm")
    tip = tip_total + tau_fixed * jnp.eye(covars, dtype=jnp.float32)
    return (sep_block[None], fill[None], sep_border[None], tip)


def solution(mesh):
    in_specs = (
        P("groups"),
        P(),
        P("groups"),
        P(None, ("groups", "tm"), None),
        P(None, ("groups", "tm"), None),
        P(None, ("groups", "tm"), None),
    )
    out_specs = (
        P(("groups", "tm"), None, None),
        P(("groups", "tm"), None, None),
        P(("groups", "tm"), None, None),
        P("groups", None),
    )
    return jax.shard_map(local, mesh=mesh, in_specs=in_specs, out_specs=out_specs, check_vma=False)
```

```python
import jax
import jax.numpy as jnp
from jax import lax
from jax.sharding import PartitionSpec as P
from jax.experimental import pallas as pl
from jax.experimental.pallas import tpu as pltpu

HIGHEST = lax.Precision.HIGHEST


def passed_along(x, axis, by):
    length = lax.axis_size(axis)
    pairs = [(i, i + by) for i in range(length) if 0 <= i + by < length]
    return lax.ppermute(x, axis, pairs)


def butterfly_sum(x, axis):
    length = lax.axis_size(axis)
    if length & (length - 1):
        return lax.psum(x, axis)
    stride = 1
    while stride < length:
        pairs = [(i, i ^ stride) for i in range(length)]
        x = x + lax.ppermute(x, axis, pairs)
        stride *= 2
    return x


def block_grid(mesh_width):
    size = 128 if mesh_width % 128 == 0 else mesh_width
    return size, mesh_width // size


def lower_blocks(matrix):
    size, count = block_grid(matrix.shape[0])
    tiles = [
        matrix[i * size : (i + 1) * size, j * size : (j + 1) * size]
        for i in range(count)
        for j in range(i + 1)
    ]
    return jnp.stack(tiles)


def from_lower_blocks(packed, mesh_width):
    size, count = block_grid(mesh_width)
    index = {}
    for i in range(count):
        for j in range(i + 1):
            index[i, j] = len(index)
    rows = []
    for i in range(count):
        row = [packed[index[i, j]] if j <= i else packed[index[j, i]].T for j in range(count)]
        rows.append(jnp.concatenate(row, axis=1))
    return jnp.concatenate(rows, axis=0)


def matmul_high(left, right):
    return jnp.dot(left, right, precision=HIGHEST)


def contract_rows(left, right):
    return lax.dot_general(
        left, right, (((0,), (0,)), ((), ())), preferred_element_type=jnp.float32
    )


def split_dot(left, right):
    dims = (((1,), (1,)), ((), ()))
    left_hi = left.astype(jnp.bfloat16)
    left_lo = (left - left_hi.astype(jnp.float32)).astype(jnp.bfloat16)
    right_hi = right.astype(jnp.bfloat16)
    right_lo = (right - right_hi.astype(jnp.float32)).astype(jnp.bfloat16)
    out = lax.dot_general(left_hi, right_hi, dims, preferred_element_type=jnp.float32)
    out = out + lax.dot_general(left_hi, right_lo, dims, preferred_element_type=jnp.float32)
    out = out + lax.dot_general(left_lo, right_hi, dims, preferred_element_type=jnp.float32)
    return out


def assemble_kernel(end_ref, packed_ref, hessian_ref, border_ref, tip_ref):
    mesh_width = hessian_ref.shape[1]
    covars = border_ref.shape[1]

    @pl.when(pl.program_id(0) == 0)
    def _():
        hessian_ref[...] = jnp.zeros_like(hessian_ref)
        border_ref[...] = jnp.zeros_like(border_ref)
        tip_ref[...] = jnp.zeros_like(tip_ref)

    chunk = packed_ref.shape[1]
    my_end = end_ref[0]
    day = packed_ref[0:1, :]
    weight = jnp.exp(packed_ref[4:5, :])
    nodes = lax.broadcasted_iota(jnp.int32, (mesh_width, chunk), 0).astype(jnp.float32)
    incidence = jnp.zeros((mesh_width, chunk), jnp.float32)
    for u in range(3):
        incidence = incidence + jnp.where(
            nodes == packed_ref[1 + u : 2 + u, :], packed_ref[5 + u : 6 + u, :], 0.0
        )
    covariate = packed_ref[8 : 8 + covars, :]
    for slot in range(2):
        chosen = jnp.where(day == my_end - slot, weight, 0.0)
        weighted = incidence * chosen
        hessian_ref[slot] += split_dot(incidence, weighted)
        border_ref[slot] += split_dot(covariate, weighted)
    tip_ref[...] += split_dot(covariate * weight, covariate)


def assemble(packed, my_end, mesh_width, covars):
    total_reads = packed.shape[1] * packed.shape[2]
    rows = packed.shape[0]
    packed = packed.reshape(rows, total_reads)
    chunk = 512 if total_reads % 512 == 0 else total_reads
    end_value = my_end.astype(jnp.float32).reshape(1)
    hessian, border, tip_data = pl.pallas_call(
        assemble_kernel,
        grid=(total_reads // chunk,),
        in_specs=[
            pl.BlockSpec(memory_space=pltpu.SMEM),
            pl.BlockSpec((rows, chunk), lambda i: (0, i)),
        ],
        out_specs=[
            pl.BlockSpec((2, mesh_width, mesh_width), lambda i: (0, 0, 0)),
            pl.BlockSpec((2, covars, mesh_width), lambda i: (0, 0, 0)),
            pl.BlockSpec((covars, covars), lambda i: (0, 0)),
        ],
        out_shape=[
            jax.ShapeDtypeStruct((2, mesh_width, mesh_width), jnp.float32),
            jax.ShapeDtypeStruct((2, covars, mesh_width), jnp.float32),
            jax.ShapeDtypeStruct((covars, covars), jnp.float32),
        ],
        compiler_params=pltpu.CompilerParams(
            dimension_semantics=("arbitrary",), vmem_limit_bytes=48 * 1024 * 1024
        ),
    )(end_value, packed)
    return (hessian, border, tip_data)


def split_parts(value):
    high = value.astype(jnp.bfloat16)
    low = (value - high.astype(jnp.float32)).astype(jnp.bfloat16)
    return high, low


def split_matmul(left, right):
    left_hi, left_lo = split_parts(left)
    right_hi, right_lo = split_parts(right)
    out = jnp.dot(left_hi, right_hi, preferred_element_type=jnp.float32)
    out = out + jnp.dot(left_hi, right_lo, preferred_element_type=jnp.float32)
    out = out + jnp.dot(left_lo, right_hi, preferred_element_type=jnp.float32)
    return out


def exact_matmul(left, right):
    return jnp.dot(left, right, precision=HIGHEST, preferred_element_type=jnp.float32)


def sweep(block_ref):
    size = block_ref.shape[0]
    lane = lax.broadcasted_iota(jnp.int32, (size, size), 1)
    sub = lax.broadcasted_iota(jnp.int32, (size, size), 0)
    lane_row = lax.broadcasted_iota(jnp.int32, (1, size), 1)

    def body(k, carry):
        current = block_ref[...]
        row = block_ref[pl.ds(k, 1), :]
        col = jnp.transpose(jnp.broadcast_to(row, (8, size)))[:, 0:1]
        pivot = jnp.sum(jnp.where(lane_row == k, row, 0.0), axis=1, keepdims=True)
        inverse = 1.0 / pivot
        scaled_row = row * inverse
        update = current - col * scaled_row
        update = jnp.where(sub == k, scaled_row, update)
        update = jnp.where(lane == k, col * inverse, update)
        update = jnp.where((sub == k) & (lane == k), -inverse, update)
        block_ref[...] = update
        return carry

    lax.fori_loop(0, size, body, 0)


def eliminate_kernel(start_ref, work_ref, solved_ref, block_ref):
    mesh_width = work_ref.shape[0]
    block_size = block_ref.shape[0]
    work_ref[...] = start_ref[...]
    for col in range(mesh_width // block_size):
        lo = col * block_size
        hi = lo + block_size
        block_ref[...] = work_ref[lo:hi, lo:hi]
        sweep(block_ref)
        solved = -exact_matmul(block_ref[...], work_ref[lo:hi, hi:])
        solved_ref[lo:hi, :] = solved[:, mesh_width - hi :]
        if hi < mesh_width:
            work_ref[hi:, hi:] = work_ref[hi:, hi:] - exact_matmul(work_ref[hi:, lo:hi], solved)


def eliminate(hessian, border, prior_diag, coupling_block):
    mesh_width = coupling_block.shape[0]
    block_size = 128 if mesh_width % 128 == 0 else mesh_width
    interior = hessian[1] + prior_diag
    start = jnp.concatenate([interior, coupling_block, border[1].T], axis=1)
    width = start.shape[1]
    work, solved = pl.pallas_call(
        eliminate_kernel,
        out_shape=[
            jax.ShapeDtypeStruct((mesh_width, width), jnp.float32),
            jax.ShapeDtypeStruct((mesh_width, width - mesh_width), jnp.float32),
        ],
        in_specs=[pl.BlockSpec(memory_space=pltpu.VMEM)],
        out_specs=[pl.BlockSpec(memory_space=pltpu.VMEM), pl.BlockSpec(memory_space=pltpu.VMEM)],
        scratch_shapes=[pltpu.VMEM((block_size, block_size), jnp.float32)],
        compiler_params=pltpu.CompilerParams(vmem_limit_bytes=60 * 1024 * 1024),
    )(start)
    schur = -lax.dot_general(
        work[:, mesh_width:], solved, (((0,), (0,)), ((), ())), precision=HIGHEST
    )
    schur_update = schur[:mesh_width, :mesh_width]
    lateral_block = schur[mesh_width:, :mesh_width]
    apex_schur_block = schur[mesh_width:, mesh_width:]
    return (schur_update, lateral_block, apex_schur_block)


def local(hyper, spatial_prec, part_lengths, reading_index, reading_value, reading_cov):
    packed = jnp.concatenate(
        [reading_index.astype(jnp.float32), reading_value, reading_cov], axis=0
    )
    packed = lax.all_to_all(packed, "tm", split_axis=2, concat_axis=1, tiled=True)
    mesh_width = spatial_prec.shape[0]
    covars = reading_cov.shape[0]
    partition_position = lax.axis_index("tm")
    corr_time = hyper[0]
    tau_field = hyper[1]
    tau_fixed = hyper[2]
    prior_diag = (1.0 + corr_time * corr_time) * tau_field * spatial_prec
    coupling_block = -corr_time * tau_field * spatial_prec
    part_ends = (jnp.cumsum(part_lengths) - 1).astype(jnp.int32)
    my_end = part_ends[partition_position]
    local_length = part_lengths[partition_position]
    hessian, border, tip_data = assemble(packed, my_end, mesh_width, covars)

    def bypass_elimination():
        return (
            jnp.zeros_like(coupling_block),
            jnp.zeros((covars, mesh_width), coupling_block.dtype),
            jnp.zeros((covars, covars), coupling_block.dtype),
        )

    def perform_elimination():
        return eliminate(hessian, border, prior_diag, coupling_block)

    schur_update, lateral_block, apex_schur_block = lax.cond(
        local_length == 2, perform_elimination, bypass_elimination
    )
    has_left = partition_position > 0
    fill = jnp.where(has_left, jnp.where(local_length == 2, schur_update, coupling_block), 0.0)
    left_update = jnp.where(has_left, schur_update, 0.0)
    left_side = jnp.where(has_left, lateral_block, 0.0)
    packed_update = lower_blocks(left_update)
    packed_update, from_right_side = passed_along((packed_update, left_side), "tm", -1)
    from_right = from_lower_blocks(packed_update, mesh_width)
    sep_block = hessian[0] + prior_diag + schur_update + from_right
    sep_border = border[0] + lateral_block + from_right_side
    tip_total = butterfly_sum(tip_data + apex_schur_block, "tm")
    tip = tip_total + tau_fixed * jnp.eye(covars, dtype=jnp.float32)
    return (sep_block[None], fill[None], sep_border[None], tip)


def solution(mesh):
    in_specs = (
        P("groups"),
        P(),
        P("groups"),
        P(None, ("groups", "tm"), None),
        P(None, ("groups", "tm"), None),
        P(None, ("groups", "tm"), None),
    )
    out_specs = (
        P(("groups", "tm"), None, None),
        P(("groups", "tm"), None, None),
        P(("groups", "tm"), None, None),
        P("groups", None),
    )
    return jax.shard_map(local, mesh=mesh, in_specs=in_specs, out_specs=out_specs, check_vma=False)
```

```python
import jax
import jax.numpy as jnp
from jax import lax
from jax.sharding import PartitionSpec as P
from jax.experimental import pallas as pl
from jax.experimental.pallas import tpu as pltpu

HIGHEST = lax.Precision.HIGHEST


def passed_along(x, axis, by):
    length = lax.axis_size(axis)
    pairs = [(i, i + by) for i in range(length) if 0 <= i + by < length]
    return lax.ppermute(x, axis, pairs)


def butterfly_sum(x, axis):
    length = lax.axis_size(axis)
    if length & (length - 1):
        return lax.psum(x, axis)
    stride = 1
    while stride < length:
        pairs = [(i, i ^ stride) for i in range(length)]
        x = x + lax.ppermute(x, axis, pairs)
        stride *= 2
    return x


def block_grid(mesh_width):
    size = 128 if mesh_width % 128 == 0 else mesh_width
    return size, mesh_width // size


def lower_blocks(matrix):
    size, count = block_grid(matrix.shape[0])
    tiles = [
        matrix[i * size : (i + 1) * size, j * size : (j + 1) * size]
        for i in range(count)
        for j in range(i + 1)
    ]
    return jnp.stack(tiles)


def from_lower_blocks(packed, mesh_width):
    size, count = block_grid(mesh_width)
    index = {}
    for i in range(count):
        for j in range(i + 1):
            index[i, j] = len(index)
    rows = []
    for i in range(count):
        row = [packed[index[i, j]] if j <= i else packed[index[j, i]].T for j in range(count)]
        rows.append(jnp.concatenate(row, axis=1))
    return jnp.concatenate(rows, axis=0)


def matmul_high(left, right):
    return jnp.dot(left, right, precision=HIGHEST)


def contract_rows(left, right):
    return lax.dot_general(
        left, right, (((0,), (0,)), ((), ())), preferred_element_type=jnp.float32
    )


def split_dot(left, right):
    dims = (((1,), (1,)), ((), ()))
    left_hi = left.astype(jnp.bfloat16)
    left_lo = (left - left_hi.astype(jnp.float32)).astype(jnp.bfloat16)
    right_hi = right.astype(jnp.bfloat16)
    right_lo = (right - right_hi.astype(jnp.float32)).astype(jnp.bfloat16)
    out = lax.dot_general(left_hi, right_hi, dims, preferred_element_type=jnp.float32)
    out = out + lax.dot_general(left_hi, right_lo, dims, preferred_element_type=jnp.float32)
    out = out + lax.dot_general(left_lo, right_hi, dims, preferred_element_type=jnp.float32)
    return out


def assemble_kernel(end_ref, packed_ref, hessian_ref, border_ref, tip_ref):
    mesh_width = hessian_ref.shape[1]
    covars = border_ref.shape[1]

    @pl.when(pl.program_id(0) == 0)
    def _():
        hessian_ref[...] = jnp.zeros_like(hessian_ref)
        border_ref[...] = jnp.zeros_like(border_ref)
        tip_ref[...] = jnp.zeros_like(tip_ref)

    chunk = packed_ref.shape[1]
    my_end = end_ref[0]
    day = packed_ref[0:1, :]
    weight = jnp.exp(packed_ref[4:5, :])
    nodes = lax.broadcasted_iota(jnp.int32, (mesh_width, chunk), 0).astype(jnp.float32)
    incidence = jnp.zeros((mesh_width, chunk), jnp.float32)
    for u in range(3):
        incidence = incidence + jnp.where(
            nodes == packed_ref[1 + u : 2 + u, :], packed_ref[5 + u : 6 + u, :], 0.0
        )
    covariate = packed_ref[8 : 8 + covars, :]
    for slot in range(2):
        chosen = jnp.where(day == my_end - slot, weight, 0.0)
        weighted = incidence * chosen
        hessian_ref[slot] += split_dot(incidence, weighted)
        border_ref[slot] += split_dot(covariate, weighted)
    tip_ref[...] += split_dot(covariate * weight, covariate)


def assemble(packed, my_end, mesh_width, covars):
    total_reads = packed.shape[1] * packed.shape[2]
    rows = packed.shape[0]
    packed = packed.reshape(rows, total_reads)
    chunk = 512 if total_reads % 512 == 0 else total_reads
    end_value = my_end.astype(jnp.float32).reshape(1)
    hessian, border, tip_data = pl.pallas_call(
        assemble_kernel,
        grid=(total_reads // chunk,),
        in_specs=[
            pl.BlockSpec(memory_space=pltpu.SMEM),
            pl.BlockSpec((rows, chunk), lambda i: (0, i)),
        ],
        out_specs=[
            pl.BlockSpec((2, mesh_width, mesh_width), lambda i: (0, 0, 0)),
            pl.BlockSpec((2, covars, mesh_width), lambda i: (0, 0, 0)),
            pl.BlockSpec((covars, covars), lambda i: (0, 0)),
        ],
        out_shape=[
            jax.ShapeDtypeStruct((2, mesh_width, mesh_width), jnp.float32),
            jax.ShapeDtypeStruct((2, covars, mesh_width), jnp.float32),
            jax.ShapeDtypeStruct((covars, covars), jnp.float32),
        ],
        compiler_params=pltpu.CompilerParams(
            dimension_semantics=("arbitrary",), vmem_limit_bytes=48 * 1024 * 1024
        ),
    )(end_value, packed)
    return (hessian, border, tip_data)


def split_parts(value):
    high = value.astype(jnp.bfloat16)
    low = (value - high.astype(jnp.float32)).astype(jnp.bfloat16)
    return high, low


def kept_split(value):
    high = lax.reduce_precision(value, exponent_bits=8, mantissa_bits=7)
    low = value - high
    return high.astype(jnp.bfloat16), low.astype(jnp.bfloat16)


def split_matmul(left, right):
    left_hi, left_lo = split_parts(left)
    right_hi, right_lo = split_parts(right)
    out = jnp.dot(left_hi, right_hi, preferred_element_type=jnp.float32)
    out = out + jnp.dot(left_hi, right_lo, preferred_element_type=jnp.float32)
    out = out + jnp.dot(left_lo, right_hi, preferred_element_type=jnp.float32)
    return out


def exact_matmul(left, right):
    return jnp.dot(left, right, precision=HIGHEST, preferred_element_type=jnp.float32)


def sweep(block_ref):
    size = block_ref.shape[0]
    lane = lax.broadcasted_iota(jnp.int32, (size, size), 1)
    sub = lax.broadcasted_iota(jnp.int32, (size, size), 0)
    lane_row = lax.broadcasted_iota(jnp.int32, (1, size), 1)

    def body(k, carry):
        current = block_ref[...]
        row = block_ref[pl.ds(k, 1), :]
        col = jnp.sum(jnp.where(lane == k, current, 0.0), axis=1, keepdims=True)
        pivot = jnp.sum(jnp.where(lane_row == k, row, 0.0), axis=1, keepdims=True)
        inverse = 1.0 / pivot
        scaled_row = row * inverse
        update = current - col * scaled_row
        update = jnp.where(sub == k, scaled_row, update)
        update = jnp.where(lane == k, col * inverse, update)
        update = jnp.where((sub == k) & (lane == k), -inverse, update)
        block_ref[...] = update
        return carry

    lax.fori_loop(0, size, body, 0)


def eliminate_kernel(start_ref, work_ref, solved_ref, block_ref):
    mesh_width = work_ref.shape[0]
    block_size = block_ref.shape[0]
    work_ref[...] = start_ref[...]
    for col in range(mesh_width // block_size):
        lo = col * block_size
        hi = lo + block_size
        block_ref[...] = work_ref[lo:hi, lo:hi]
        sweep(block_ref)
        solved = -exact_matmul(block_ref[...], work_ref[lo:hi, hi:])
        solved_ref[lo:hi, :] = solved[:, mesh_width - hi :]
        if hi < mesh_width:
            work_ref[hi:, hi:] = work_ref[hi:, hi:] - exact_matmul(work_ref[hi:, lo:hi], solved)


def eliminate(hessian, border, prior_diag, coupling_block):
    mesh_width = coupling_block.shape[0]
    block_size = 128 if mesh_width % 128 == 0 else mesh_width
    interior = hessian[1] + prior_diag
    start = jnp.concatenate([interior, coupling_block, border[1].T], axis=1)
    width = start.shape[1]
    work, solved = pl.pallas_call(
        eliminate_kernel,
        out_shape=[
            jax.ShapeDtypeStruct((mesh_width, width), jnp.float32),
            jax.ShapeDtypeStruct((mesh_width, width - mesh_width), jnp.float32),
        ],
        in_specs=[pl.BlockSpec(memory_space=pltpu.VMEM)],
        out_specs=[pl.BlockSpec(memory_space=pltpu.VMEM), pl.BlockSpec(memory_space=pltpu.VMEM)],
        scratch_shapes=[pltpu.VMEM((block_size, block_size), jnp.float32)],
        compiler_params=pltpu.CompilerParams(vmem_limit_bytes=60 * 1024 * 1024),
    )(start)
    rhs_hi, rhs_lo = kept_split(work[:, mesh_width:])
    solved_hi, solved_lo = kept_split(solved)
    schur = -(
        contract_rows(rhs_hi, solved_hi)
        + contract_rows(rhs_hi, solved_lo)
        + contract_rows(rhs_lo, solved_hi)
    )
    schur_update = schur[:mesh_width, :mesh_width]
    lateral_block = schur[mesh_width:, :mesh_width]
    apex_schur_block = schur[mesh_width:, mesh_width:]
    return (schur_update, lateral_block, apex_schur_block)


def local(hyper, spatial_prec, part_lengths, reading_index, reading_value, reading_cov):
    packed = jnp.concatenate(
        [reading_index.astype(jnp.float32), reading_value, reading_cov], axis=0
    )
    packed = lax.all_to_all(packed, "tm", split_axis=2, concat_axis=1, tiled=True)
    mesh_width = spatial_prec.shape[0]
    covars = reading_cov.shape[0]
    partition_position = lax.axis_index("tm")
    corr_time = hyper[0]
    tau_field = hyper[1]
    tau_fixed = hyper[2]
    prior_diag = (1.0 + corr_time * corr_time) * tau_field * spatial_prec
    coupling_block = -corr_time * tau_field * spatial_prec
    part_ends = (jnp.cumsum(part_lengths) - 1).astype(jnp.int32)
    my_end = part_ends[partition_position]
    local_length = part_lengths[partition_position]
    hessian, border, tip_data = assemble(packed, my_end, mesh_width, covars)

    def bypass_elimination():
        return (
            jnp.zeros_like(coupling_block),
            jnp.zeros((covars, mesh_width), coupling_block.dtype),
            jnp.zeros((covars, covars), coupling_block.dtype),
        )

    def perform_elimination():
        return eliminate(hessian, border, prior_diag, coupling_block)

    schur_update, lateral_block, apex_schur_block = lax.cond(
        local_length == 2, perform_elimination, bypass_elimination
    )
    has_left = partition_position > 0
    fill = jnp.where(has_left, jnp.where(local_length == 2, schur_update, coupling_block), 0.0)
    left_update = jnp.where(has_left, schur_update, 0.0)
    left_side = jnp.where(has_left, lateral_block, 0.0)
    packed_update = lower_blocks(left_update)
    packed_update, from_right_side = passed_along((packed_update, left_side), "tm", -1)
    from_right = from_lower_blocks(packed_update, mesh_width)
    sep_block = hessian[0] + prior_diag + schur_update + from_right
    sep_border = border[0] + lateral_block + from_right_side
    tip_total = butterfly_sum(tip_data + apex_schur_block, "tm")
    tip = tip_total + tau_fixed * jnp.eye(covars, dtype=jnp.float32)
    return (sep_block[None], fill[None], sep_border[None], tip)


def solution(mesh):
    in_specs = (
        P("groups"),
        P(),
        P("groups"),
        P(None, ("groups", "tm"), None),
        P(None, ("groups", "tm"), None),
        P(None, ("groups", "tm"), None),
    )
    out_specs = (
        P(("groups", "tm"), None, None),
        P(("groups", "tm"), None, None),
        P(("groups", "tm"), None, None),
        P("groups", None),
    )
    return jax.shard_map(local, mesh=mesh, in_specs=in_specs, out_specs=out_specs, check_vma=False)
```

```python
import jax
import jax.numpy as jnp
from jax import lax
from jax.sharding import PartitionSpec as P
from jax.experimental import pallas as pl
from jax.experimental.pallas import tpu as pltpu

HIGHEST = lax.Precision.HIGHEST


def passed_along(x, axis, by):
    length = lax.axis_size(axis)
    pairs = [(i, i + by) for i in range(length) if 0 <= i + by < length]
    return lax.ppermute(x, axis, pairs)


def butterfly_sum(x, axis):
    length = lax.axis_size(axis)
    if length & (length - 1):
        return lax.psum(x, axis)
    stride = 1
    while stride < length:
        pairs = [(i, i ^ stride) for i in range(length)]
        x = x + lax.ppermute(x, axis, pairs)
        stride *= 2
    return x


def block_grid(mesh_width):
    size = 128 if mesh_width % 128 == 0 else mesh_width
    return size, mesh_width // size


def lower_blocks(matrix):
    size, count = block_grid(matrix.shape[0])
    tiles = [
        matrix[i * size : (i + 1) * size, j * size : (j + 1) * size]
        for i in range(count)
        for j in range(i + 1)
    ]
    return jnp.stack(tiles)


def from_lower_blocks(packed, mesh_width):
    size, count = block_grid(mesh_width)
    index = {}
    for i in range(count):
        for j in range(i + 1):
            index[i, j] = len(index)
    rows = []
    for i in range(count):
        row = [packed[index[i, j]] if j <= i else packed[index[j, i]].T for j in range(count)]
        rows.append(jnp.concatenate(row, axis=1))
    return jnp.concatenate(rows, axis=0)


def matmul_high(left, right):
    return jnp.dot(left, right, precision=HIGHEST)


def contract_rows(left, right):
    return lax.dot_general(
        left, right, (((0,), (0,)), ((), ())), preferred_element_type=jnp.float32
    )


def split_dot(left, right):
    dims = (((1,), (1,)), ((), ()))
    left_hi = left.astype(jnp.bfloat16)
    left_lo = (left - left_hi.astype(jnp.float32)).astype(jnp.bfloat16)
    right_hi = right.astype(jnp.bfloat16)
    right_lo = (right - right_hi.astype(jnp.float32)).astype(jnp.bfloat16)
    out = lax.dot_general(left_hi, right_hi, dims, preferred_element_type=jnp.float32)
    out = out + lax.dot_general(left_hi, right_lo, dims, preferred_element_type=jnp.float32)
    out = out + lax.dot_general(left_lo, right_hi, dims, preferred_element_type=jnp.float32)
    return out


def assemble_kernel(end_ref, packed_ref, hessian_ref, border_ref, tip_ref):
    mesh_width = hessian_ref.shape[1]
    covars = border_ref.shape[1]

    @pl.when(pl.program_id(0) == 0)
    def _():
        hessian_ref[...] = jnp.zeros_like(hessian_ref)
        border_ref[...] = jnp.zeros_like(border_ref)
        tip_ref[...] = jnp.zeros_like(tip_ref)

    chunk = packed_ref.shape[1]
    my_end = end_ref[0]
    day = packed_ref[0:1, :]
    weight = jnp.exp(packed_ref[4:5, :])
    nodes = lax.broadcasted_iota(jnp.int32, (mesh_width, chunk), 0).astype(jnp.float32)
    incidence = jnp.zeros((mesh_width, chunk), jnp.float32)
    for u in range(3):
        incidence = incidence + jnp.where(
            nodes == packed_ref[1 + u : 2 + u, :], packed_ref[5 + u : 6 + u, :], 0.0
        )
    covariate = packed_ref[8 : 8 + covars, :]
    for slot in range(2):
        chosen = jnp.where(day == my_end - slot, weight, 0.0)
        weighted = incidence * chosen
        hessian_ref[slot] += split_dot(incidence, weighted)
        border_ref[slot] += split_dot(covariate, weighted)
    tip_ref[...] += split_dot(covariate * weight, covariate)


def assemble(packed, my_end, mesh_width, covars):
    total_reads = packed.shape[1] * packed.shape[2]
    rows = packed.shape[0]
    packed = packed.reshape(rows, total_reads)
    chunk = 512 if total_reads % 512 == 0 else total_reads
    end_value = my_end.astype(jnp.float32).reshape(1)
    hessian, border, tip_data = pl.pallas_call(
        assemble_kernel,
        grid=(total_reads // chunk,),
        in_specs=[
            pl.BlockSpec(memory_space=pltpu.SMEM),
            pl.BlockSpec((rows, chunk), lambda i: (0, i)),
        ],
        out_specs=[
            pl.BlockSpec((2, mesh_width, mesh_width), lambda i: (0, 0, 0)),
            pl.BlockSpec((2, covars, mesh_width), lambda i: (0, 0, 0)),
            pl.BlockSpec((covars, covars), lambda i: (0, 0)),
        ],
        out_shape=[
            jax.ShapeDtypeStruct((2, mesh_width, mesh_width), jnp.float32),
            jax.ShapeDtypeStruct((2, covars, mesh_width), jnp.float32),
            jax.ShapeDtypeStruct((covars, covars), jnp.float32),
        ],
        compiler_params=pltpu.CompilerParams(
            dimension_semantics=("arbitrary",), vmem_limit_bytes=48 * 1024 * 1024
        ),
    )(end_value, packed)
    return (hessian, border, tip_data)


def split_parts(value):
    high = value.astype(jnp.bfloat16)
    low = (value - high.astype(jnp.float32)).astype(jnp.bfloat16)
    return high, low


def kept_split(value):
    high = lax.reduce_precision(value, exponent_bits=8, mantissa_bits=7)
    low = value - high
    return high.astype(jnp.bfloat16), low.astype(jnp.bfloat16)


def split_matmul(left, right):
    left_hi, left_lo = split_parts(left)
    right_hi, right_lo = split_parts(right)
    out = jnp.dot(left_hi, right_hi, preferred_element_type=jnp.float32)
    out = out + jnp.dot(left_hi, right_lo, preferred_element_type=jnp.float32)
    out = out + jnp.dot(left_lo, right_hi, preferred_element_type=jnp.float32)
    return out


def exact_matmul(left, right):
    return jnp.dot(left, right, precision=HIGHEST, preferred_element_type=jnp.float32)


def sweep(block_ref):
    size = block_ref.shape[0]
    lane = lax.broadcasted_iota(jnp.int32, (size, size), 1)
    sub = lax.broadcasted_iota(jnp.int32, (size, size), 0)
    lane_row = lax.broadcasted_iota(jnp.int32, (1, size), 1)

    def body(k, carry):
        current = block_ref[...]
        row = block_ref[pl.ds(k, 1), :]
        col = jnp.sum(jnp.where(lane == k, current, 0.0), axis=1, keepdims=True)
        pivot = jnp.sum(jnp.where(lane_row == k, row, 0.0), axis=1, keepdims=True)
        inverse = 1.0 / pivot
        scaled_row = row * inverse
        update = current - col * scaled_row
        update = jnp.where(sub == k, scaled_row, update)
        update = jnp.where(lane == k, col * inverse, update)
        update = jnp.where((sub == k) & (lane == k), -inverse, update)
        block_ref[...] = update
        return carry

    lax.fori_loop(0, size, body, 0)


def eliminate_kernel(start_ref, work_ref, solved_ref, block_ref):
    mesh_width = work_ref.shape[0]
    block_size = block_ref.shape[0]
    work_ref[...] = start_ref[...]
    for col in range(mesh_width // block_size):
        lo = col * block_size
        hi = lo + block_size
        block_ref[...] = work_ref[lo:hi, lo:hi]
        sweep(block_ref)
        solved = -split_matmul(block_ref[...], work_ref[lo:hi, hi:])
        solved_ref[lo:hi, :] = solved[:, mesh_width - hi :]
        if hi < mesh_width:
            work_ref[hi:, hi:] = work_ref[hi:, hi:] - split_matmul(work_ref[hi:, lo:hi], solved)


def eliminate(hessian, border, prior_diag, coupling_block):
    mesh_width = coupling_block.shape[0]
    block_size = 128 if mesh_width % 128 == 0 else mesh_width
    interior = hessian[1] + prior_diag
    start = jnp.concatenate([interior, coupling_block, border[1].T], axis=1)
    width = start.shape[1]
    work, solved = pl.pallas_call(
        eliminate_kernel,
        out_shape=[
            jax.ShapeDtypeStruct((mesh_width, width), jnp.float32),
            jax.ShapeDtypeStruct((mesh_width, width - mesh_width), jnp.float32),
        ],
        in_specs=[pl.BlockSpec(memory_space=pltpu.VMEM)],
        out_specs=[pl.BlockSpec(memory_space=pltpu.VMEM), pl.BlockSpec(memory_space=pltpu.VMEM)],
        scratch_shapes=[pltpu.VMEM((block_size, block_size), jnp.float32)],
        compiler_params=pltpu.CompilerParams(vmem_limit_bytes=60 * 1024 * 1024),
    )(start)
    rhs_hi, rhs_lo = kept_split(work[:, mesh_width:])
    solved_hi, solved_lo = kept_split(solved)
    schur = -(
        contract_rows(rhs_hi, solved_hi)
        + contract_rows(rhs_hi, solved_lo)
        + contract_rows(rhs_lo, solved_hi)
    )
    schur_update = schur[:mesh_width, :mesh_width]
    lateral_block = schur[mesh_width:, :mesh_width]
    apex_schur_block = schur[mesh_width:, mesh_width:]
    return (schur_update, lateral_block, apex_schur_block)


def local(hyper, spatial_prec, part_lengths, reading_index, reading_value, reading_cov):
    packed = jnp.concatenate(
        [reading_index.astype(jnp.float32), reading_value, reading_cov], axis=0
    )
    packed = lax.all_to_all(packed, "tm", split_axis=2, concat_axis=1, tiled=True)
    mesh_width = spatial_prec.shape[0]
    covars = reading_cov.shape[0]
    partition_position = lax.axis_index("tm")
    corr_time = hyper[0]
    tau_field = hyper[1]
    tau_fixed = hyper[2]
    prior_diag = (1.0 + corr_time * corr_time) * tau_field * spatial_prec
    coupling_block = -corr_time * tau_field * spatial_prec
    part_ends = (jnp.cumsum(part_lengths) - 1).astype(jnp.int32)
    my_end = part_ends[partition_position]
    local_length = part_lengths[partition_position]
    hessian, border, tip_data = assemble(packed, my_end, mesh_width, covars)

    def bypass_elimination():
        return (
            jnp.zeros_like(coupling_block),
            jnp.zeros((covars, mesh_width), coupling_block.dtype),
            jnp.zeros((covars, covars), coupling_block.dtype),
        )

    def perform_elimination():
        return eliminate(hessian, border, prior_diag, coupling_block)

    schur_update, lateral_block, apex_schur_block = lax.cond(
        local_length == 2, perform_elimination, bypass_elimination
    )
    has_left = partition_position > 0
    fill = jnp.where(has_left, jnp.where(local_length == 2, schur_update, coupling_block), 0.0)
    left_update = jnp.where(has_left, schur_update, 0.0)
    left_side = jnp.where(has_left, lateral_block, 0.0)
    packed_update = lower_blocks(left_update)
    packed_update, from_right_side = passed_along((packed_update, left_side), "tm", -1)
    from_right = from_lower_blocks(packed_update, mesh_width)
    sep_block = hessian[0] + prior_diag + schur_update + from_right
    sep_border = border[0] + lateral_block + from_right_side
    tip_total = butterfly_sum(tip_data + apex_schur_block, "tm")
    tip = tip_total + tau_fixed * jnp.eye(covars, dtype=jnp.float32)
    return (sep_block[None], fill[None], sep_border[None], tip)


def solution(mesh):
    in_specs = (
        P("groups"),
        P(),
        P("groups"),
        P(None, ("groups", "tm"), None),
        P(None, ("groups", "tm"), None),
        P(None, ("groups", "tm"), None),
    )
    out_specs = (
        P(("groups", "tm"), None, None),
        P(("groups", "tm"), None, None),
        P(("groups", "tm"), None, None),
        P("groups", None),
    )
    return jax.shard_map(local, mesh=mesh, in_specs=in_specs, out_specs=out_specs, check_vma=False)
```

```python
import jax
import jax.numpy as jnp
from jax import lax
from jax.sharding import PartitionSpec as P
from jax.experimental import pallas as pl
from jax.experimental.pallas import tpu as pltpu

HIGHEST = lax.Precision.HIGHEST


def passed_along(x, axis, by):
    length = lax.axis_size(axis)
    pairs = [(i, i + by) for i in range(length) if 0 <= i + by < length]
    return lax.ppermute(x, axis, pairs)


def butterfly_sum(x, axis):
    length = lax.axis_size(axis)
    if length & (length - 1):
        return lax.psum(x, axis)
    strides = [1]
    while strides[-1] * 2 < length:
        strides.append(strides[-1] * 2)
    for stride in [1] + strides[:0:-1]:
        pairs = [(i, i ^ stride) for i in range(length)]
        x = x + lax.ppermute(x, axis, pairs)
    return x


def block_grid(mesh_width):
    size = 128 if mesh_width % 128 == 0 else mesh_width
    return size, mesh_width // size


def lower_blocks(matrix):
    size, count = block_grid(matrix.shape[0])
    tiles = [
        matrix[i * size : (i + 1) * size, j * size : (j + 1) * size]
        for i in range(count)
        for j in range(i + 1)
    ]
    return jnp.stack(tiles)


def from_lower_blocks(packed, mesh_width):
    size, count = block_grid(mesh_width)
    index = {}
    for i in range(count):
        for j in range(i + 1):
            index[i, j] = len(index)
    rows = []
    for i in range(count):
        row = [packed[index[i, j]] if j <= i else packed[index[j, i]].T for j in range(count)]
        rows.append(jnp.concatenate(row, axis=1))
    return jnp.concatenate(rows, axis=0)


def matmul_high(left, right):
    return jnp.dot(left, right, precision=HIGHEST)


def contract_rows(left, right):
    return lax.dot_general(
        left, right, (((0,), (0,)), ((), ())), preferred_element_type=jnp.float32
    )


def split_dot(left, right):
    dims = (((1,), (1,)), ((), ()))
    left_hi = left.astype(jnp.bfloat16)
    left_lo = (left - left_hi.astype(jnp.float32)).astype(jnp.bfloat16)
    right_hi = right.astype(jnp.bfloat16)
    right_lo = (right - right_hi.astype(jnp.float32)).astype(jnp.bfloat16)
    out = lax.dot_general(left_hi, right_hi, dims, preferred_element_type=jnp.float32)
    out = out + lax.dot_general(left_hi, right_lo, dims, preferred_element_type=jnp.float32)
    out = out + lax.dot_general(left_lo, right_hi, dims, preferred_element_type=jnp.float32)
    return out


def assemble_kernel(end_ref, packed_ref, hessian_ref, border_ref, tip_ref):
    mesh_width = hessian_ref.shape[1]
    covars = border_ref.shape[1]

    @pl.when(pl.program_id(0) == 0)
    def _():
        hessian_ref[...] = jnp.zeros_like(hessian_ref)
        border_ref[...] = jnp.zeros_like(border_ref)
        tip_ref[...] = jnp.zeros_like(tip_ref)

    chunk = packed_ref.shape[1]
    my_end = end_ref[0]
    day = packed_ref[0:1, :]
    weight = jnp.exp(packed_ref[4:5, :])
    nodes = lax.broadcasted_iota(jnp.int32, (mesh_width, chunk), 0).astype(jnp.float32)
    incidence = jnp.zeros((mesh_width, chunk), jnp.float32)
    for u in range(3):
        incidence = incidence + jnp.where(
            nodes == packed_ref[1 + u : 2 + u, :], packed_ref[5 + u : 6 + u, :], 0.0
        )
    covariate = packed_ref[8 : 8 + covars, :]
    for slot in range(2):
        chosen = jnp.where(day == my_end - slot, weight, 0.0)
        weighted = incidence * chosen
        hessian_ref[slot] += split_dot(incidence, weighted)
        border_ref[slot] += split_dot(covariate, weighted)
    tip_ref[...] += split_dot(covariate * weight, covariate)


def assemble(packed, my_end, mesh_width, covars):
    total_reads = packed.shape[1] * packed.shape[2]
    rows = packed.shape[0]
    packed = packed.reshape(rows, total_reads)
    chunk = 512 if total_reads % 512 == 0 else total_reads
    end_value = my_end.astype(jnp.float32).reshape(1)
    hessian, border, tip_data = pl.pallas_call(
        assemble_kernel,
        grid=(total_reads // chunk,),
        in_specs=[
            pl.BlockSpec(memory_space=pltpu.SMEM),
            pl.BlockSpec((rows, chunk), lambda i: (0, i)),
        ],
        out_specs=[
            pl.BlockSpec((2, mesh_width, mesh_width), lambda i: (0, 0, 0)),
            pl.BlockSpec((2, covars, mesh_width), lambda i: (0, 0, 0)),
            pl.BlockSpec((covars, covars), lambda i: (0, 0)),
        ],
        out_shape=[
            jax.ShapeDtypeStruct((2, mesh_width, mesh_width), jnp.float32),
            jax.ShapeDtypeStruct((2, covars, mesh_width), jnp.float32),
            jax.ShapeDtypeStruct((covars, covars), jnp.float32),
        ],
        compiler_params=pltpu.CompilerParams(
            dimension_semantics=("arbitrary",), vmem_limit_bytes=48 * 1024 * 1024
        ),
    )(end_value, packed)
    return (hessian, border, tip_data)


def split_parts(value):
    high = value.astype(jnp.bfloat16)
    low = (value - high.astype(jnp.float32)).astype(jnp.bfloat16)
    return high, low


def kept_split(value):
    high = lax.reduce_precision(value, exponent_bits=8, mantissa_bits=7)
    low = value - high
    return high.astype(jnp.bfloat16), low.astype(jnp.bfloat16)


def split_matmul(left, right):
    left_hi, left_lo = split_parts(left)
    right_hi, right_lo = split_parts(right)
    out = jnp.dot(left_hi, right_hi, preferred_element_type=jnp.float32)
    out = out + jnp.dot(left_hi, right_lo, preferred_element_type=jnp.float32)
    out = out + jnp.dot(left_lo, right_hi, preferred_element_type=jnp.float32)
    return out


def exact_matmul(left, right):
    return jnp.dot(left, right, precision=HIGHEST, preferred_element_type=jnp.float32)


def sweep(block_ref):
    size = block_ref.shape[0]
    lane = lax.broadcasted_iota(jnp.int32, (size, size), 1)
    sub = lax.broadcasted_iota(jnp.int32, (size, size), 0)
    lane_row = lax.broadcasted_iota(jnp.int32, (1, size), 1)

    def body(k, carry):
        current = block_ref[...]
        row = block_ref[pl.ds(k, 1), :]
        col = jnp.sum(jnp.where(lane == k, current, 0.0), axis=1, keepdims=True)
        pivot = jnp.sum(jnp.where(lane_row == k, row, 0.0), axis=1, keepdims=True)
        inverse = 1.0 / pivot
        scaled_row = row * inverse
        update = current - col * scaled_row
        update = jnp.where(sub == k, scaled_row, update)
        update = jnp.where(lane == k, col * inverse, update)
        update = jnp.where((sub == k) & (lane == k), -inverse, update)
        block_ref[...] = update
        return carry

    lax.fori_loop(0, size, body, 0)


def eliminate_kernel(start_ref, work_ref, solved_ref, block_ref):
    mesh_width = work_ref.shape[0]
    block_size = block_ref.shape[0]
    work_ref[...] = start_ref[...]
    for col in range(mesh_width // block_size):
        lo = col * block_size
        hi = lo + block_size
        block_ref[...] = work_ref[lo:hi, lo:hi]
        sweep(block_ref)
        solved = -split_matmul(block_ref[...], work_ref[lo:hi, hi:])
        solved_ref[lo:hi, :] = solved[:, mesh_width - hi :]
        if hi < mesh_width:
            work_ref[hi:, hi:] = work_ref[hi:, hi:] - split_matmul(work_ref[hi:, lo:hi], solved)


def eliminate(hessian, border, prior_diag, coupling_block):
    mesh_width = coupling_block.shape[0]
    block_size = 128 if mesh_width % 128 == 0 else mesh_width
    interior = hessian[1] + prior_diag
    start = jnp.concatenate([interior, coupling_block, border[1].T], axis=1)
    width = start.shape[1]
    work, solved = pl.pallas_call(
        eliminate_kernel,
        out_shape=[
            jax.ShapeDtypeStruct((mesh_width, width), jnp.float32),
            jax.ShapeDtypeStruct((mesh_width, width - mesh_width), jnp.float32),
        ],
        in_specs=[pl.BlockSpec(memory_space=pltpu.VMEM)],
        out_specs=[pl.BlockSpec(memory_space=pltpu.VMEM), pl.BlockSpec(memory_space=pltpu.VMEM)],
        scratch_shapes=[pltpu.VMEM((block_size, block_size), jnp.float32)],
        compiler_params=pltpu.CompilerParams(vmem_limit_bytes=60 * 1024 * 1024),
    )(start)
    rhs_hi, rhs_lo = kept_split(work[:, mesh_width:])
    solved_hi, solved_lo = kept_split(solved)
    schur = -(
        contract_rows(rhs_hi, solved_hi)
        + contract_rows(rhs_hi, solved_lo)
        + contract_rows(rhs_lo, solved_hi)
    )
    schur_update = schur[:mesh_width, :mesh_width]
    lateral_block = schur[mesh_width:, :mesh_width]
    apex_schur_block = schur[mesh_width:, mesh_width:]
    return (schur_update, lateral_block, apex_schur_block)


def local(hyper, spatial_prec, part_lengths, reading_index, reading_value, reading_cov):
    packed = jnp.concatenate(
        [reading_index.astype(jnp.float32), reading_value, reading_cov], axis=0
    )
    packed = lax.all_to_all(packed, "tm", split_axis=2, concat_axis=1, tiled=True)
    mesh_width = spatial_prec.shape[0]
    covars = reading_cov.shape[0]
    partition_position = lax.axis_index("tm")
    corr_time = hyper[0]
    tau_field = hyper[1]
    tau_fixed = hyper[2]
    prior_diag = (1.0 + corr_time * corr_time) * tau_field * spatial_prec
    coupling_block = -corr_time * tau_field * spatial_prec
    part_ends = (jnp.cumsum(part_lengths) - 1).astype(jnp.int32)
    my_end = part_ends[partition_position]
    local_length = part_lengths[partition_position]
    hessian, border, tip_data = assemble(packed, my_end, mesh_width, covars)

    def bypass_elimination():
        return (
            jnp.zeros_like(coupling_block),
            jnp.zeros((covars, mesh_width), coupling_block.dtype),
            jnp.zeros((covars, covars), coupling_block.dtype),
        )

    def perform_elimination():
        return eliminate(hessian, border, prior_diag, coupling_block)

    schur_update, lateral_block, apex_schur_block = lax.cond(
        local_length == 2, perform_elimination, bypass_elimination
    )
    has_left = partition_position > 0
    fill = jnp.where(has_left, jnp.where(local_length == 2, schur_update, coupling_block), 0.0)
    left_update = jnp.where(has_left, schur_update, 0.0)
    left_side = jnp.where(has_left, lateral_block, 0.0)
    packed_update = lower_blocks(left_update)
    packed_update, from_right_side = passed_along((packed_update, left_side), "tm", -1)
    from_right = from_lower_blocks(packed_update, mesh_width)
    sep_block = hessian[0] + prior_diag + schur_update + from_right
    sep_border = border[0] + lateral_block + from_right_side
    tip_total = butterfly_sum(tip_data + apex_schur_block, "tm")
    tip = tip_total + tau_fixed * jnp.eye(covars, dtype=jnp.float32)
    return (sep_block[None], fill[None], sep_border[None], tip)


def solution(mesh):
    in_specs = (
        P("groups"),
        P(),
        P("groups"),
        P(None, ("groups", "tm"), None),
        P(None, ("groups", "tm"), None),
        P(None, ("groups", "tm"), None),
    )
    out_specs = (
        P(("groups", "tm"), None, None),
        P(("groups", "tm"), None, None),
        P(("groups", "tm"), None, None),
        P("groups", None),
    )
    return jax.shard_map(local, mesh=mesh, in_specs=in_specs, out_specs=out_specs, check_vma=False)
```

```python
import jax
import jax.numpy as jnp
from jax import lax
from jax.sharding import PartitionSpec as P
from jax.experimental import pallas as pl
from jax.experimental.pallas import tpu as pltpu

HIGHEST = lax.Precision.HIGHEST


def passed_along(x, axis, by):
    length = lax.axis_size(axis)
    pairs = [(i, i + by) for i in range(length) if 0 <= i + by < length]
    return lax.ppermute(x, axis, pairs)


def butterfly_sum(x, axis):
    length = lax.axis_size(axis)
    if length & (length - 1):
        return lax.psum(x, axis)
    stride = 1
    while stride < length:
        pairs = [(i, i ^ stride) for i in range(length)]
        x = x + lax.ppermute(x, axis, pairs)
        stride *= 2
    return x


def block_grid(mesh_width):
    size = 128 if mesh_width % 128 == 0 else mesh_width
    return size, mesh_width // size


def lower_blocks(matrix):
    size, count = block_grid(matrix.shape[0])
    tiles = [
        matrix[i * size : (i + 1) * size, j * size : (j + 1) * size]
        for i in range(count)
        for j in range(i + 1)
    ]
    return jnp.stack(tiles)


def from_lower_blocks(packed, mesh_width):
    size, count = block_grid(mesh_width)
    index = {}
    for i in range(count):
        for j in range(i + 1):
            index[i, j] = len(index)
    rows = []
    for i in range(count):
        row = [packed[index[i, j]] if j <= i else packed[index[j, i]].T for j in range(count)]
        rows.append(jnp.concatenate(row, axis=1))
    return jnp.concatenate(rows, axis=0)


def matmul_high(left, right):
    return jnp.dot(left, right, precision=HIGHEST)


def contract_rows(left, right):
    return lax.dot_general(
        left, right, (((0,), (0,)), ((), ())), preferred_element_type=jnp.float32
    )


def split_dot(left, right):
    dims = (((1,), (1,)), ((), ()))
    left_hi = left.astype(jnp.bfloat16)
    left_lo = (left - left_hi.astype(jnp.float32)).astype(jnp.bfloat16)
    right_hi = right.astype(jnp.bfloat16)
    right_lo = (right - right_hi.astype(jnp.float32)).astype(jnp.bfloat16)
    out = lax.dot_general(left_hi, right_hi, dims, preferred_element_type=jnp.float32)
    out = out + lax.dot_general(left_hi, right_lo, dims, preferred_element_type=jnp.float32)
    out = out + lax.dot_general(left_lo, right_hi, dims, preferred_element_type=jnp.float32)
    return out


def assemble_kernel(end_ref, packed_ref, hessian_ref, border_ref, tip_ref):
    mesh_width = hessian_ref.shape[1]
    covars = border_ref.shape[1]

    @pl.when(pl.program_id(0) == 0)
    def _():
        hessian_ref[...] = jnp.zeros_like(hessian_ref)
        border_ref[...] = jnp.zeros_like(border_ref)
        tip_ref[...] = jnp.zeros_like(tip_ref)

    chunk = packed_ref.shape[1]
    my_end = end_ref[0]
    day = packed_ref[0:1, :]
    weight = jnp.exp(packed_ref[4:5, :])
    nodes = lax.broadcasted_iota(jnp.int32, (mesh_width, chunk), 0).astype(jnp.float32)
    incidence = jnp.zeros((mesh_width, chunk), jnp.float32)
    for u in range(3):
        incidence = incidence + jnp.where(
            nodes == packed_ref[1 + u : 2 + u, :], packed_ref[5 + u : 6 + u, :], 0.0
        )
    covariate = packed_ref[8 : 8 + covars, :]
    for slot in range(2):
        chosen = jnp.where(day == my_end - slot, weight, 0.0)
        weighted = incidence * chosen
        hessian_ref[slot] += split_dot(incidence, weighted)
        border_ref[slot] += split_dot(covariate, weighted)
    tip_ref[...] += split_dot(covariate * weight, covariate)


def assemble(packed, my_end, mesh_width, covars):
    total_reads = packed.shape[1] * packed.shape[2]
    rows = packed.shape[0]
    packed = packed.reshape(rows, total_reads)
    chunk = 512 if total_reads % 512 == 0 else total_reads
    end_value = my_end.astype(jnp.float32).reshape(1)
    hessian, border, tip_data = pl.pallas_call(
        assemble_kernel,
        grid=(total_reads // chunk,),
        in_specs=[
            pl.BlockSpec(memory_space=pltpu.SMEM),
            pl.BlockSpec((rows, chunk), lambda i: (0, i)),
        ],
        out_specs=[
            pl.BlockSpec((2, mesh_width, mesh_width), lambda i: (0, 0, 0)),
            pl.BlockSpec((2, covars, mesh_width), lambda i: (0, 0, 0)),
            pl.BlockSpec((covars, covars), lambda i: (0, 0)),
        ],
        out_shape=[
            jax.ShapeDtypeStruct((2, mesh_width, mesh_width), jnp.float32),
            jax.ShapeDtypeStruct((2, covars, mesh_width), jnp.float32),
            jax.ShapeDtypeStruct((covars, covars), jnp.float32),
        ],
        compiler_params=pltpu.CompilerParams(
            dimension_semantics=("arbitrary",), vmem_limit_bytes=48 * 1024 * 1024
        ),
    )(end_value, packed)
    return (hessian, border, tip_data)


def split_parts(value):
    high = value.astype(jnp.bfloat16)
    low = (value - high.astype(jnp.float32)).astype(jnp.bfloat16)
    return high, low


def kept_split(value):
    high = lax.reduce_precision(value, exponent_bits=8, mantissa_bits=7)
    low = value - high
    return high.astype(jnp.bfloat16), low.astype(jnp.bfloat16)


def split_matmul(left, right):
    left_hi, left_lo = split_parts(left)
    right_hi, right_lo = split_parts(right)
    out = jnp.dot(left_hi, right_hi, preferred_element_type=jnp.float32)
    out = out + jnp.dot(left_hi, right_lo, preferred_element_type=jnp.float32)
    out = out + jnp.dot(left_lo, right_hi, preferred_element_type=jnp.float32)
    return out


def exact_matmul(left, right):
    return jnp.dot(left, right, precision=HIGHEST, preferred_element_type=jnp.float32)


def sweep(block_ref):
    size = block_ref.shape[0]
    lane = lax.broadcasted_iota(jnp.int32, (size, size), 1)
    sub = lax.broadcasted_iota(jnp.int32, (size, size), 0)
    lane_row = lax.broadcasted_iota(jnp.int32, (1, size), 1)

    def body(k, current):
        row = jnp.sum(jnp.where(sub == k, current, 0.0), axis=0, keepdims=True)
        col = jnp.sum(jnp.where(lane == k, current, 0.0), axis=1, keepdims=True)
        pivot = jnp.sum(jnp.where(lane_row == k, row, 0.0), axis=1, keepdims=True)
        inverse = 1.0 / pivot
        scaled_row = row * inverse
        update = current - col * scaled_row
        update = jnp.where(sub == k, scaled_row, update)
        update = jnp.where(lane == k, col * inverse, update)
        return jnp.where((sub == k) & (lane == k), -inverse, update)

    block_ref[...] = lax.fori_loop(0, size, body, block_ref[...])


def eliminate_kernel(start_ref, work_ref, solved_ref, block_ref):
    mesh_width = work_ref.shape[0]
    block_size = block_ref.shape[0]
    work_ref[...] = start_ref[...]
    for col in range(mesh_width // block_size):
        lo = col * block_size
        hi = lo + block_size
        block_ref[...] = work_ref[lo:hi, lo:hi]
        sweep(block_ref)
        solved = -split_matmul(block_ref[...], work_ref[lo:hi, hi:])
        solved_ref[lo:hi, :] = solved[:, mesh_width - hi :]
        if hi < mesh_width:
            work_ref[hi:, hi:] = work_ref[hi:, hi:] - split_matmul(work_ref[hi:, lo:hi], solved)


def eliminate(hessian, border, prior_diag, coupling_block):
    mesh_width = coupling_block.shape[0]
    block_size = 128 if mesh_width % 128 == 0 else mesh_width
    interior = hessian[1] + prior_diag
    start = jnp.concatenate([interior, coupling_block, border[1].T], axis=1)
    width = start.shape[1]
    work, solved = pl.pallas_call(
        eliminate_kernel,
        out_shape=[
            jax.ShapeDtypeStruct((mesh_width, width), jnp.float32),
            jax.ShapeDtypeStruct((mesh_width, width - mesh_width), jnp.float32),
        ],
        in_specs=[pl.BlockSpec(memory_space=pltpu.VMEM)],
        out_specs=[pl.BlockSpec(memory_space=pltpu.VMEM), pl.BlockSpec(memory_space=pltpu.VMEM)],
        scratch_shapes=[pltpu.VMEM((block_size, block_size), jnp.float32)],
        compiler_params=pltpu.CompilerParams(vmem_limit_bytes=60 * 1024 * 1024),
    )(start)
    rhs_hi, rhs_lo = kept_split(work[:, mesh_width:])
    solved_hi, solved_lo = kept_split(solved)
    schur = -(
        contract_rows(rhs_hi, solved_hi)
        + contract_rows(rhs_hi, solved_lo)
        + contract_rows(rhs_lo, solved_hi)
    )
    schur_update = schur[:mesh_width, :mesh_width]
    lateral_block = schur[mesh_width:, :mesh_width]
    apex_schur_block = schur[mesh_width:, mesh_width:]
    return (schur_update, lateral_block, apex_schur_block)


def local(hyper, spatial_prec, part_lengths, reading_index, reading_value, reading_cov):
    packed = jnp.concatenate(
        [reading_index.astype(jnp.float32), reading_value, reading_cov], axis=0
    )
    packed = lax.all_to_all(packed, "tm", split_axis=2, concat_axis=1, tiled=True)
    mesh_width = spatial_prec.shape[0]
    covars = reading_cov.shape[0]
    partition_position = lax.axis_index("tm")
    corr_time = hyper[0]
    tau_field = hyper[1]
    tau_fixed = hyper[2]
    prior_diag = (1.0 + corr_time * corr_time) * tau_field * spatial_prec
    coupling_block = -corr_time * tau_field * spatial_prec
    part_ends = (jnp.cumsum(part_lengths) - 1).astype(jnp.int32)
    my_end = part_ends[partition_position]
    local_length = part_lengths[partition_position]
    hessian, border, tip_data = assemble(packed, my_end, mesh_width, covars)

    def bypass_elimination():
        return (
            jnp.zeros_like(coupling_block),
            jnp.zeros((covars, mesh_width), coupling_block.dtype),
            jnp.zeros((covars, covars), coupling_block.dtype),
        )

    def perform_elimination():
        return eliminate(hessian, border, prior_diag, coupling_block)

    schur_update, lateral_block, apex_schur_block = lax.cond(
        local_length == 2, perform_elimination, bypass_elimination
    )
    has_left = partition_position > 0
    fill = jnp.where(has_left, jnp.where(local_length == 2, schur_update, coupling_block), 0.0)
    left_update = jnp.where(has_left, schur_update, 0.0)
    left_side = jnp.where(has_left, lateral_block, 0.0)
    packed_update = lower_blocks(left_update)
    packed_update, from_right_side = passed_along((packed_update, left_side), "tm", -1)
    from_right = from_lower_blocks(packed_update, mesh_width)
    sep_block = hessian[0] + prior_diag + schur_update + from_right
    sep_border = border[0] + lateral_block + from_right_side
    tip_total = butterfly_sum(tip_data + apex_schur_block, "tm")
    tip = tip_total + tau_fixed * jnp.eye(covars, dtype=jnp.float32)
    return (sep_block[None], fill[None], sep_border[None], tip)


def solution(mesh):
    in_specs = (
        P("groups"),
        P(),
        P("groups"),
        P(None, ("groups", "tm"), None),
        P(None, ("groups", "tm"), None),
        P(None, ("groups", "tm"), None),
    )
    out_specs = (
        P(("groups", "tm"), None, None),
        P(("groups", "tm"), None, None),
        P(("groups", "tm"), None, None),
        P("groups", None),
    )
    return jax.shard_map(local, mesh=mesh, in_specs=in_specs, out_specs=out_specs, check_vma=False)
```

```python
import jax
import jax.numpy as jnp
from jax import lax
from jax.sharding import PartitionSpec as P
from jax.experimental import pallas as pl
from jax.experimental.pallas import tpu as pltpu

HIGHEST = lax.Precision.HIGHEST


def passed_along(x, axis, by):
    length = lax.axis_size(axis)
    pairs = [(i, i + by) for i in range(length) if 0 <= i + by < length]
    return lax.ppermute(x, axis, pairs)


def butterfly_sum(x, axis):
    length = lax.axis_size(axis)
    if length & (length - 1):
        return lax.psum(x, axis)
    stride = 1
    while stride < length:
        pairs = [(i, i ^ stride) for i in range(length)]
        x = x + lax.ppermute(x, axis, pairs)
        stride *= 2
    return x


def block_grid(mesh_width):
    size = 128 if mesh_width % 128 == 0 else mesh_width
    return size, mesh_width // size


def lower_blocks(matrix):
    size, count = block_grid(matrix.shape[0])
    tiles = [
        matrix[i * size : (i + 1) * size, j * size : (j + 1) * size]
        for i in range(count)
        for j in range(i + 1)
    ]
    return jnp.stack(tiles)


def from_lower_blocks(packed, mesh_width):
    size, count = block_grid(mesh_width)
    index = {}
    for i in range(count):
        for j in range(i + 1):
            index[i, j] = len(index)
    rows = []
    for i in range(count):
        row = [packed[index[i, j]] if j <= i else packed[index[j, i]].T for j in range(count)]
        rows.append(jnp.concatenate(row, axis=1))
    return jnp.concatenate(rows, axis=0)


def matmul_high(left, right):
    return jnp.dot(left, right, precision=HIGHEST)


def contract_rows(left, right):
    return lax.dot_general(
        left, right, (((0,), (0,)), ((), ())), preferred_element_type=jnp.float32
    )


def split_dot(left, right):
    dims = (((1,), (1,)), ((), ()))
    left_hi = left.astype(jnp.bfloat16)
    left_lo = (left - left_hi.astype(jnp.float32)).astype(jnp.bfloat16)
    right_hi = right.astype(jnp.bfloat16)
    right_lo = (right - right_hi.astype(jnp.float32)).astype(jnp.bfloat16)
    out = lax.dot_general(left_hi, right_hi, dims, preferred_element_type=jnp.float32)
    out = out + lax.dot_general(left_hi, right_lo, dims, preferred_element_type=jnp.float32)
    out = out + lax.dot_general(left_lo, right_hi, dims, preferred_element_type=jnp.float32)
    return out


def assemble_kernel(end_ref, packed_ref, hessian_ref, border_ref, tip_ref):
    mesh_width = hessian_ref.shape[1]
    covars = border_ref.shape[1]

    @pl.when(pl.program_id(0) == 0)
    def _():
        hessian_ref[...] = jnp.zeros_like(hessian_ref)
        border_ref[...] = jnp.zeros_like(border_ref)
        tip_ref[...] = jnp.zeros_like(tip_ref)

    chunk = packed_ref.shape[1]
    my_end = end_ref[0]
    day = packed_ref[0:1, :]
    weight = jnp.exp(packed_ref[4:5, :])
    nodes = lax.broadcasted_iota(jnp.int32, (mesh_width, chunk), 0).astype(jnp.float32)
    incidence = jnp.zeros((mesh_width, chunk), jnp.float32)
    for u in range(3):
        incidence = incidence + jnp.where(
            nodes == packed_ref[1 + u : 2 + u, :], packed_ref[5 + u : 6 + u, :], 0.0
        )
    covariate = packed_ref[8 : 8 + covars, :]
    for slot in range(2):
        chosen = jnp.where(day == my_end - slot, weight, 0.0)
        weighted = incidence * chosen
        hessian_ref[slot] += split_dot(incidence, weighted)
        border_ref[slot] += split_dot(covariate, weighted)
    tip_ref[...] += split_dot(covariate * weight, covariate)


def assemble(packed, my_end, mesh_width, covars):
    total_reads = packed.shape[1] * packed.shape[2]
    rows = packed.shape[0]
    packed = packed.reshape(rows, total_reads)
    chunk = 1024 if total_reads % 1024 == 0 else total_reads
    end_value = my_end.astype(jnp.float32).reshape(1)
    hessian, border, tip_data = pl.pallas_call(
        assemble_kernel,
        grid=(total_reads // chunk,),
        in_specs=[
            pl.BlockSpec(memory_space=pltpu.SMEM),
            pl.BlockSpec((rows, chunk), lambda i: (0, i)),
        ],
        out_specs=[
            pl.BlockSpec((2, mesh_width, mesh_width), lambda i: (0, 0, 0)),
            pl.BlockSpec((2, covars, mesh_width), lambda i: (0, 0, 0)),
            pl.BlockSpec((covars, covars), lambda i: (0, 0)),
        ],
        out_shape=[
            jax.ShapeDtypeStruct((2, mesh_width, mesh_width), jnp.float32),
            jax.ShapeDtypeStruct((2, covars, mesh_width), jnp.float32),
            jax.ShapeDtypeStruct((covars, covars), jnp.float32),
        ],
        compiler_params=pltpu.CompilerParams(
            dimension_semantics=("arbitrary",), vmem_limit_bytes=48 * 1024 * 1024
        ),
    )(end_value, packed)
    return (hessian, border, tip_data)


def split_parts(value):
    high = value.astype(jnp.bfloat16)
    low = (value - high.astype(jnp.float32)).astype(jnp.bfloat16)
    return high, low


def kept_split(value):
    high = lax.reduce_precision(value, exponent_bits=8, mantissa_bits=7)
    low = value - high
    return high.astype(jnp.bfloat16), low.astype(jnp.bfloat16)


def split_matmul(left, right):
    left_hi, left_lo = split_parts(left)
    right_hi, right_lo = split_parts(right)
    out = jnp.dot(left_hi, right_hi, preferred_element_type=jnp.float32)
    out = out + jnp.dot(left_hi, right_lo, preferred_element_type=jnp.float32)
    out = out + jnp.dot(left_lo, right_hi, preferred_element_type=jnp.float32)
    return out


def exact_matmul(left, right):
    return jnp.dot(left, right, precision=HIGHEST, preferred_element_type=jnp.float32)


def sweep(block_ref):
    size = block_ref.shape[0]
    lane = lax.broadcasted_iota(jnp.int32, (size, size), 1)
    sub = lax.broadcasted_iota(jnp.int32, (size, size), 0)
    lane_row = lax.broadcasted_iota(jnp.int32, (1, size), 1)

    def body(k, carry):
        current = block_ref[...]
        row = block_ref[pl.ds(k, 1), :]
        col = jnp.sum(jnp.where(lane == k, current, 0.0), axis=1, keepdims=True)
        pivot = jnp.sum(jnp.where(lane_row == k, row, 0.0), axis=1, keepdims=True)
        inverse = 1.0 / pivot
        scaled_row = row * inverse
        update = current - col * scaled_row
        update = jnp.where(sub == k, scaled_row, update)
        update = jnp.where(lane == k, col * inverse, update)
        update = jnp.where((sub == k) & (lane == k), -inverse, update)
        block_ref[...] = update
        return carry

    lax.fori_loop(0, size, body, 0)


def eliminate_kernel(start_ref, work_ref, solved_ref, block_ref):
    mesh_width = work_ref.shape[0]
    block_size = block_ref.shape[0]
    work_ref[...] = start_ref[...]
    for col in range(mesh_width // block_size):
        lo = col * block_size
        hi = lo + block_size
        block_ref[...] = work_ref[lo:hi, lo:hi]
        sweep(block_ref)
        solved = -split_matmul(block_ref[...], work_ref[lo:hi, hi:])
        solved_ref[lo:hi, :] = solved[:, mesh_width - hi :]
        if hi < mesh_width:
            work_ref[hi:, hi:] = work_ref[hi:, hi:] - split_matmul(work_ref[hi:, lo:hi], solved)


def eliminate(hessian, border, prior_diag, coupling_block):
    mesh_width = coupling_block.shape[0]
    block_size = 128 if mesh_width % 128 == 0 else mesh_width
    interior = hessian[1] + prior_diag
    start = jnp.concatenate([interior, coupling_block, border[1].T], axis=1)
    width = start.shape[1]
    work, solved = pl.pallas_call(
        eliminate_kernel,
        out_shape=[
            jax.ShapeDtypeStruct((mesh_width, width), jnp.float32),
            jax.ShapeDtypeStruct((mesh_width, width - mesh_width), jnp.float32),
        ],
        in_specs=[pl.BlockSpec(memory_space=pltpu.VMEM)],
        out_specs=[pl.BlockSpec(memory_space=pltpu.VMEM), pl.BlockSpec(memory_space=pltpu.VMEM)],
        scratch_shapes=[pltpu.VMEM((block_size, block_size), jnp.float32)],
        compiler_params=pltpu.CompilerParams(vmem_limit_bytes=60 * 1024 * 1024),
    )(start)
    rhs_hi, rhs_lo = kept_split(work[:, mesh_width:])
    solved_hi, solved_lo = kept_split(solved)
    schur = -(
        contract_rows(rhs_hi, solved_hi)
        + contract_rows(rhs_hi, solved_lo)
        + contract_rows(rhs_lo, solved_hi)
    )
    schur_update = schur[:mesh_width, :mesh_width]
    lateral_block = schur[mesh_width:, :mesh_width]
    apex_schur_block = schur[mesh_width:, mesh_width:]
    return (schur_update, lateral_block, apex_schur_block)


def local(hyper, spatial_prec, part_lengths, reading_index, reading_value, reading_cov):
    packed = jnp.concatenate(
        [reading_index.astype(jnp.float32), reading_value, reading_cov], axis=0
    )
    packed = lax.all_to_all(packed, "tm", split_axis=2, concat_axis=1, tiled=True)
    mesh_width = spatial_prec.shape[0]
    covars = reading_cov.shape[0]
    partition_position = lax.axis_index("tm")
    corr_time = hyper[0]
    tau_field = hyper[1]
    tau_fixed = hyper[2]
    prior_diag = (1.0 + corr_time * corr_time) * tau_field * spatial_prec
    coupling_block = -corr_time * tau_field * spatial_prec
    part_ends = (jnp.cumsum(part_lengths) - 1).astype(jnp.int32)
    my_end = part_ends[partition_position]
    local_length = part_lengths[partition_position]
    hessian, border, tip_data = assemble(packed, my_end, mesh_width, covars)

    def bypass_elimination():
        return (
            jnp.zeros_like(coupling_block),
            jnp.zeros((covars, mesh_width), coupling_block.dtype),
            jnp.zeros((covars, covars), coupling_block.dtype),
        )

    def perform_elimination():
        return eliminate(hessian, border, prior_diag, coupling_block)

    schur_update, lateral_block, apex_schur_block = lax.cond(
        local_length == 2, perform_elimination, bypass_elimination
    )
    has_left = partition_position > 0
    fill = jnp.where(has_left, jnp.where(local_length == 2, schur_update, coupling_block), 0.0)
    left_update = jnp.where(has_left, schur_update, 0.0)
    left_side = jnp.where(has_left, lateral_block, 0.0)
    packed_update = lower_blocks(left_update)
    packed_update, from_right_side = passed_along((packed_update, left_side), "tm", -1)
    from_right = from_lower_blocks(packed_update, mesh_width)
    sep_block = hessian[0] + prior_diag + schur_update + from_right
    sep_border = border[0] + lateral_block + from_right_side
    tip_total = butterfly_sum(tip_data + apex_schur_block, "tm")
    tip = tip_total + tau_fixed * jnp.eye(covars, dtype=jnp.float32)
    return (sep_block[None], fill[None], sep_border[None], tip)


def solution(mesh):
    in_specs = (
        P("groups"),
        P(),
        P("groups"),
        P(None, ("groups", "tm"), None),
        P(None, ("groups", "tm"), None),
        P(None, ("groups", "tm"), None),
    )
    out_specs = (
        P(("groups", "tm"), None, None),
        P(("groups", "tm"), None, None),
        P(("groups", "tm"), None, None),
        P("groups", None),
    )
    return jax.shard_map(local, mesh=mesh, in_specs=in_specs, out_specs=out_specs, check_vma=False)
```

```python
import jax
import jax.numpy as jnp
from jax import lax
from jax.sharding import PartitionSpec as P
from jax.experimental import pallas as pl
from jax.experimental.pallas import tpu as pltpu

HIGHEST = lax.Precision.HIGHEST


def passed_along(x, axis, by):
    length = lax.axis_size(axis)
    pairs = [(i, i + by) for i in range(length) if 0 <= i + by < length]
    return lax.ppermute(x, axis, pairs)


def butterfly_sum(x, axis):
    length = lax.axis_size(axis)
    if length & (length - 1):
        return lax.psum(x, axis)
    stride = 1
    while stride < length:
        pairs = [(i, i ^ stride) for i in range(length)]
        x = x + lax.ppermute(x, axis, pairs)
        stride *= 2
    return x


def block_grid(mesh_width):
    size = 128 if mesh_width % 128 == 0 else mesh_width
    return size, mesh_width // size


def lower_blocks(matrix):
    size, count = block_grid(matrix.shape[0])
    tiles = [
        matrix[i * size : (i + 1) * size, j * size : (j + 1) * size]
        for i in range(count)
        for j in range(i + 1)
    ]
    return jnp.stack(tiles)


def from_lower_blocks(packed, mesh_width):
    size, count = block_grid(mesh_width)
    index = {}
    for i in range(count):
        for j in range(i + 1):
            index[i, j] = len(index)
    rows = []
    for i in range(count):
        row = [packed[index[i, j]] if j <= i else packed[index[j, i]].T for j in range(count)]
        rows.append(jnp.concatenate(row, axis=1))
    return jnp.concatenate(rows, axis=0)


def matmul_high(left, right):
    return jnp.dot(left, right, precision=HIGHEST)


def contract_rows(left, right):
    return lax.dot_general(
        left, right, (((0,), (0,)), ((), ())), preferred_element_type=jnp.float32
    )


def split_dot(left, right):
    dims = (((1,), (1,)), ((), ()))
    left_hi = left.astype(jnp.bfloat16)
    left_lo = (left - left_hi.astype(jnp.float32)).astype(jnp.bfloat16)
    right_hi = right.astype(jnp.bfloat16)
    right_lo = (right - right_hi.astype(jnp.float32)).astype(jnp.bfloat16)
    out = lax.dot_general(left_hi, right_hi, dims, preferred_element_type=jnp.float32)
    out = out + lax.dot_general(left_hi, right_lo, dims, preferred_element_type=jnp.float32)
    out = out + lax.dot_general(left_lo, right_hi, dims, preferred_element_type=jnp.float32)
    return out


def assemble_kernel(end_ref, packed_ref, hessian_ref, border_ref, tip_ref):
    mesh_width = hessian_ref.shape[1]
    covars = border_ref.shape[1]

    @pl.when(pl.program_id(0) == 0)
    def _():
        hessian_ref[...] = jnp.zeros_like(hessian_ref)
        border_ref[...] = jnp.zeros_like(border_ref)
        tip_ref[...] = jnp.zeros_like(tip_ref)

    chunk = packed_ref.shape[1]
    my_end = end_ref[0]
    day = packed_ref[0:1, :]
    weight = jnp.exp(packed_ref[4:5, :])
    nodes = lax.broadcasted_iota(jnp.int32, (mesh_width, chunk), 0).astype(jnp.float32)
    incidence = jnp.zeros((mesh_width, chunk), jnp.float32)
    for u in range(3):
        incidence = incidence + jnp.where(
            nodes == packed_ref[1 + u : 2 + u, :], packed_ref[5 + u : 6 + u, :], 0.0
        )
    covariate = packed_ref[8 : 8 + covars, :]
    for slot in range(2):
        chosen = jnp.where(day == my_end - slot, weight, 0.0)
        weighted = incidence * chosen
        hessian_ref[slot] += split_dot(incidence, weighted)
        border_ref[slot] += split_dot(covariate, weighted)
    tip_ref[...] += split_dot(covariate * weight, covariate)


def assemble(packed, my_end, mesh_width, covars):
    total_reads = packed.shape[1] * packed.shape[2]
    rows = packed.shape[0]
    packed = packed.reshape(rows, total_reads)
    chunk = 1024 if total_reads % 1024 == 0 else total_reads
    end_value = my_end.astype(jnp.float32).reshape(1)
    hessian, border, tip_data = pl.pallas_call(
        assemble_kernel,
        grid=(total_reads // chunk,),
        in_specs=[
            pl.BlockSpec(memory_space=pltpu.SMEM),
            pl.BlockSpec((rows, chunk), lambda i: (0, i)),
        ],
        out_specs=[
            pl.BlockSpec((2, mesh_width, mesh_width), lambda i: (0, 0, 0)),
            pl.BlockSpec((2, covars, mesh_width), lambda i: (0, 0, 0)),
            pl.BlockSpec((covars, covars), lambda i: (0, 0)),
        ],
        out_shape=[
            jax.ShapeDtypeStruct((2, mesh_width, mesh_width), jnp.float32),
            jax.ShapeDtypeStruct((2, covars, mesh_width), jnp.float32),
            jax.ShapeDtypeStruct((covars, covars), jnp.float32),
        ],
        compiler_params=pltpu.CompilerParams(
            dimension_semantics=("arbitrary",), vmem_limit_bytes=48 * 1024 * 1024
        ),
    )(end_value, packed)
    return (hessian, border, tip_data)


def split_parts(value):
    high = value.astype(jnp.bfloat16)
    low = (value - high.astype(jnp.float32)).astype(jnp.bfloat16)
    return high, low


def kept_split(value):
    high = lax.reduce_precision(value, exponent_bits=8, mantissa_bits=7)
    low = value - high
    return high.astype(jnp.bfloat16), low.astype(jnp.bfloat16)


def split_matmul(left, right):
    left_hi, left_lo = split_parts(left)
    right_hi, right_lo = split_parts(right)
    out = jnp.dot(left_hi, right_hi, preferred_element_type=jnp.float32)
    out = out + jnp.dot(left_hi, right_lo, preferred_element_type=jnp.float32)
    out = out + jnp.dot(left_lo, right_hi, preferred_element_type=jnp.float32)
    return out


def exact_matmul(left, right):
    return jnp.dot(left, right, precision=HIGHEST, preferred_element_type=jnp.float32)


def sweep(block_ref):
    size = block_ref.shape[0]
    lane = lax.broadcasted_iota(jnp.int32, (size, size), 1)
    sub = lax.broadcasted_iota(jnp.int32, (size, size), 0)
    lane_row = lax.broadcasted_iota(jnp.int32, (1, size), 1)

    def body(k, carry):
        current = block_ref[...]
        row = block_ref[pl.ds(k, 1), :]
        col = jnp.sum(jnp.where(lane == k, current, 0.0), axis=1, keepdims=True)
        pivot = jnp.sum(jnp.where(lane_row == k, row, 0.0), axis=1, keepdims=True)
        inverse = 1.0 / pivot
        scaled_row = row * inverse
        update = current - col * scaled_row
        fixed_row = jnp.where(lane_row == k, -inverse, scaled_row)
        update = jnp.where(lane == k, col * inverse, update)
        update = jnp.where(sub == k, fixed_row, update)
        block_ref[...] = update
        return carry

    lax.fori_loop(0, size, body, 0)


def eliminate_kernel(start_ref, work_ref, solved_ref, block_ref):
    mesh_width = work_ref.shape[0]
    block_size = block_ref.shape[0]
    work_ref[...] = start_ref[...]
    for col in range(mesh_width // block_size):
        lo = col * block_size
        hi = lo + block_size
        block_ref[...] = work_ref[lo:hi, lo:hi]
        sweep(block_ref)
        solved = -split_matmul(block_ref[...], work_ref[lo:hi, hi:])
        solved_ref[lo:hi, :] = solved[:, mesh_width - hi :]
        if hi < mesh_width:
            work_ref[hi:, hi:] = work_ref[hi:, hi:] - split_matmul(work_ref[hi:, lo:hi], solved)


def eliminate(hessian, border, prior_diag, coupling_block):
    mesh_width = coupling_block.shape[0]
    block_size = 128 if mesh_width % 128 == 0 else mesh_width
    interior = hessian[1] + prior_diag
    start = jnp.concatenate([interior, coupling_block, border[1].T], axis=1)
    width = start.shape[1]
    work, solved = pl.pallas_call(
        eliminate_kernel,
        out_shape=[
            jax.ShapeDtypeStruct((mesh_width, width), jnp.float32),
            jax.ShapeDtypeStruct((mesh_width, width - mesh_width), jnp.float32),
        ],
        in_specs=[pl.BlockSpec(memory_space=pltpu.VMEM)],
        out_specs=[pl.BlockSpec(memory_space=pltpu.VMEM), pl.BlockSpec(memory_space=pltpu.VMEM)],
        scratch_shapes=[pltpu.VMEM((block_size, block_size), jnp.float32)],
        compiler_params=pltpu.CompilerParams(vmem_limit_bytes=60 * 1024 * 1024),
    )(start)
    rhs_hi, rhs_lo = kept_split(work[:, mesh_width:])
    solved_hi, solved_lo = kept_split(solved)
    schur = -(
        contract_rows(rhs_hi, solved_hi)
        + contract_rows(rhs_hi, solved_lo)
        + contract_rows(rhs_lo, solved_hi)
    )
    schur_update = schur[:mesh_width, :mesh_width]
    lateral_block = schur[mesh_width:, :mesh_width]
    apex_schur_block = schur[mesh_width:, mesh_width:]
    return (schur_update, lateral_block, apex_schur_block)


def local(hyper, spatial_prec, part_lengths, reading_index, reading_value, reading_cov):
    packed = jnp.concatenate(
        [reading_index.astype(jnp.float32), reading_value, reading_cov], axis=0
    )
    packed = lax.all_to_all(packed, "tm", split_axis=2, concat_axis=1, tiled=True)
    mesh_width = spatial_prec.shape[0]
    covars = reading_cov.shape[0]
    partition_position = lax.axis_index("tm")
    corr_time = hyper[0]
    tau_field = hyper[1]
    tau_fixed = hyper[2]
    prior_diag = (1.0 + corr_time * corr_time) * tau_field * spatial_prec
    coupling_block = -corr_time * tau_field * spatial_prec
    part_ends = (jnp.cumsum(part_lengths) - 1).astype(jnp.int32)
    my_end = part_ends[partition_position]
    local_length = part_lengths[partition_position]
    hessian, border, tip_data = assemble(packed, my_end, mesh_width, covars)

    def bypass_elimination():
        return (
            jnp.zeros_like(coupling_block),
            jnp.zeros((covars, mesh_width), coupling_block.dtype),
            jnp.zeros((covars, covars), coupling_block.dtype),
        )

    def perform_elimination():
        return eliminate(hessian, border, prior_diag, coupling_block)

    schur_update, lateral_block, apex_schur_block = lax.cond(
        local_length == 2, perform_elimination, bypass_elimination
    )
    has_left = partition_position > 0
    fill = jnp.where(has_left, jnp.where(local_length == 2, schur_update, coupling_block), 0.0)
    left_update = jnp.where(has_left, schur_update, 0.0)
    left_side = jnp.where(has_left, lateral_block, 0.0)
    packed_update = lower_blocks(left_update)
    packed_update, from_right_side = passed_along((packed_update, left_side), "tm", -1)
    from_right = from_lower_blocks(packed_update, mesh_width)
    sep_block = hessian[0] + prior_diag + schur_update + from_right
    sep_border = border[0] + lateral_block + from_right_side
    tip_total = butterfly_sum(tip_data + apex_schur_block, "tm")
    tip = tip_total + tau_fixed * jnp.eye(covars, dtype=jnp.float32)
    return (sep_block[None], fill[None], sep_border[None], tip)


def solution(mesh):
    in_specs = (
        P("groups"),
        P(),
        P("groups"),
        P(None, ("groups", "tm"), None),
        P(None, ("groups", "tm"), None),
        P(None, ("groups", "tm"), None),
    )
    out_specs = (
        P(("groups", "tm"), None, None),
        P(("groups", "tm"), None, None),
        P(("groups", "tm"), None, None),
        P("groups", None),
    )
    return jax.shard_map(local, mesh=mesh, in_specs=in_specs, out_specs=out_specs, check_vma=False)
```

```python
import jax
import jax.numpy as jnp
from jax import lax
from jax.sharding import PartitionSpec as P
from jax.experimental import pallas as pl
from jax.experimental.pallas import tpu as pltpu

HIGHEST = lax.Precision.HIGHEST


def passed_along(x, axis, by):
    length = lax.axis_size(axis)
    pairs = [(i, i + by) for i in range(length) if 0 <= i + by < length]
    return lax.ppermute(x, axis, pairs)


def butterfly_sum(x, axis):
    length = lax.axis_size(axis)
    if length & (length - 1):
        return lax.psum(x, axis)
    stride = 1
    while stride < length:
        pairs = [(i, i ^ stride) for i in range(length)]
        x = x + lax.ppermute(x, axis, pairs)
        stride *= 2
    return x


def block_grid(mesh_width):
    size = 128 if mesh_width % 128 == 0 else mesh_width
    return size, mesh_width // size


def lower_blocks(matrix):
    size, count = block_grid(matrix.shape[0])
    tiles = [
        matrix[i * size : (i + 1) * size, j * size : (j + 1) * size]
        for i in range(count)
        for j in range(i + 1)
    ]
    return jnp.stack(tiles)


def from_lower_blocks(packed, mesh_width):
    size, count = block_grid(mesh_width)
    index = {}
    for i in range(count):
        for j in range(i + 1):
            index[i, j] = len(index)
    rows = []
    for i in range(count):
        row = [packed[index[i, j]] if j <= i else packed[index[j, i]].T for j in range(count)]
        rows.append(jnp.concatenate(row, axis=1))
    return jnp.concatenate(rows, axis=0)


def matmul_high(left, right):
    return jnp.dot(left, right, precision=HIGHEST)


def contract_rows(left, right):
    return lax.dot_general(
        left, right, (((0,), (0,)), ((), ())), preferred_element_type=jnp.float32
    )


def split_dot(left, right):
    dims = (((1,), (1,)), ((), ()))
    left_hi = left.astype(jnp.bfloat16)
    left_lo = (left - left_hi.astype(jnp.float32)).astype(jnp.bfloat16)
    right_hi = right.astype(jnp.bfloat16)
    right_lo = (right - right_hi.astype(jnp.float32)).astype(jnp.bfloat16)
    out = lax.dot_general(left_hi, right_hi, dims, preferred_element_type=jnp.float32)
    out = out + lax.dot_general(left_hi, right_lo, dims, preferred_element_type=jnp.float32)
    out = out + lax.dot_general(left_lo, right_hi, dims, preferred_element_type=jnp.float32)
    return out


def assemble_kernel(end_ref, packed_ref, hessian_ref, border_ref, tip_ref):
    mesh_width = hessian_ref.shape[1]
    covars = border_ref.shape[1]

    @pl.when(pl.program_id(0) == 0)
    def _():
        hessian_ref[...] = jnp.zeros_like(hessian_ref)
        border_ref[...] = jnp.zeros_like(border_ref)
        tip_ref[...] = jnp.zeros_like(tip_ref)

    chunk = packed_ref.shape[1]
    my_end = end_ref[0]
    day = packed_ref[0:1, :]
    weight = jnp.exp(packed_ref[4:5, :])
    nodes = lax.broadcasted_iota(jnp.int32, (mesh_width, chunk), 0).astype(jnp.float32)
    incidence = jnp.zeros((mesh_width, chunk), jnp.float32)
    for u in range(3):
        incidence = incidence + jnp.where(
            nodes == packed_ref[1 + u : 2 + u, :], packed_ref[5 + u : 6 + u, :], 0.0
        )
    covariate = packed_ref[8 : 8 + covars, :]
    for slot in range(2):
        chosen = jnp.where(day == my_end - slot, weight, 0.0)
        weighted = incidence * chosen
        hessian_ref[slot] += split_dot(incidence, weighted)
        border_ref[slot] += split_dot(covariate, weighted)
    tip_ref[...] += split_dot(covariate * weight, covariate)


def assemble(packed, my_end, mesh_width, covars):
    total_reads = packed.shape[1] * packed.shape[2]
    rows = packed.shape[0]
    packed = packed.reshape(rows, total_reads)
    chunk = 1024 if total_reads % 1024 == 0 else total_reads
    end_value = my_end.astype(jnp.float32).reshape(1)
    hessian, border, tip_data = pl.pallas_call(
        assemble_kernel,
        grid=(total_reads // chunk,),
        in_specs=[
            pl.BlockSpec(memory_space=pltpu.SMEM),
            pl.BlockSpec((rows, chunk), lambda i: (0, i)),
        ],
        out_specs=[
            pl.BlockSpec((2, mesh_width, mesh_width), lambda i: (0, 0, 0)),
            pl.BlockSpec((2, covars, mesh_width), lambda i: (0, 0, 0)),
            pl.BlockSpec((covars, covars), lambda i: (0, 0)),
        ],
        out_shape=[
            jax.ShapeDtypeStruct((2, mesh_width, mesh_width), jnp.float32),
            jax.ShapeDtypeStruct((2, covars, mesh_width), jnp.float32),
            jax.ShapeDtypeStruct((covars, covars), jnp.float32),
        ],
        compiler_params=pltpu.CompilerParams(
            dimension_semantics=("arbitrary",), vmem_limit_bytes=48 * 1024 * 1024
        ),
    )(end_value, packed)
    return (hessian, border, tip_data)


def split_parts(value):
    high = value.astype(jnp.bfloat16)
    low = (value - high.astype(jnp.float32)).astype(jnp.bfloat16)
    return high, low


def kept_split(value):
    high = lax.reduce_precision(value, exponent_bits=8, mantissa_bits=7)
    low = value - high
    return high.astype(jnp.bfloat16), low.astype(jnp.bfloat16)


def split_matmul(left, right):
    left_hi, left_lo = split_parts(left)
    right_hi, right_lo = split_parts(right)
    out = jnp.dot(left_hi, right_hi, preferred_element_type=jnp.float32)
    out = out + jnp.dot(left_hi, right_lo, preferred_element_type=jnp.float32)
    out = out + jnp.dot(left_lo, right_hi, preferred_element_type=jnp.float32)
    return out


def exact_matmul(left, right):
    return jnp.dot(left, right, precision=HIGHEST, preferred_element_type=jnp.float32)


def sweep(block_ref):
    size = block_ref.shape[0]
    lane = lax.broadcasted_iota(jnp.int32, (size, size), 1)
    sub = lax.broadcasted_iota(jnp.int32, (size, size), 0)
    lane_row = lax.broadcasted_iota(jnp.int32, (1, size), 1)

    def body(k, carry):
        current = block_ref[...]
        row = block_ref[pl.ds(k, 1), :]
        col = jnp.sum(jnp.where(lane == k, current, 0.0), axis=1, keepdims=True)
        pivot = jnp.sum(jnp.where(lane_row == k, row, 0.0), axis=1, keepdims=True)
        inverse = 1.0 / pivot
        scaled_row = row * inverse
        update = current - col * scaled_row
        fixed_row = jnp.where(lane_row == k, -inverse, scaled_row)
        update = jnp.where(lane == k, col * inverse, update)
        update = jnp.where(sub == k, fixed_row, update)
        block_ref[...] = update
        return carry

    lax.fori_loop(0, size, body, 0, unroll=2)


def eliminate_kernel(start_ref, work_ref, solved_ref, block_ref):
    mesh_width = work_ref.shape[0]
    block_size = block_ref.shape[0]
    work_ref[...] = start_ref[...]
    for col in range(mesh_width // block_size):
        lo = col * block_size
        hi = lo + block_size
        block_ref[...] = work_ref[lo:hi, lo:hi]
        sweep(block_ref)
        solved = -split_matmul(block_ref[...], work_ref[lo:hi, hi:])
        solved_ref[lo:hi, :] = solved[:, mesh_width - hi :]
        if hi < mesh_width:
            work_ref[hi:, hi:] = work_ref[hi:, hi:] - split_matmul(work_ref[hi:, lo:hi], solved)


def eliminate(hessian, border, prior_diag, coupling_block):
    mesh_width = coupling_block.shape[0]
    block_size = 128 if mesh_width % 128 == 0 else mesh_width
    interior = hessian[1] + prior_diag
    start = jnp.concatenate([interior, coupling_block, border[1].T], axis=1)
    width = start.shape[1]
    work, solved = pl.pallas_call(
        eliminate_kernel,
        out_shape=[
            jax.ShapeDtypeStruct((mesh_width, width), jnp.float32),
            jax.ShapeDtypeStruct((mesh_width, width - mesh_width), jnp.float32),
        ],
        in_specs=[pl.BlockSpec(memory_space=pltpu.VMEM)],
        out_specs=[pl.BlockSpec(memory_space=pltpu.VMEM), pl.BlockSpec(memory_space=pltpu.VMEM)],
        scratch_shapes=[pltpu.VMEM((block_size, block_size), jnp.float32)],
        compiler_params=pltpu.CompilerParams(vmem_limit_bytes=60 * 1024 * 1024),
    )(start)
    rhs_hi, rhs_lo = kept_split(work[:, mesh_width:])
    solved_hi, solved_lo = kept_split(solved)
    schur = -(
        contract_rows(rhs_hi, solved_hi)
        + contract_rows(rhs_hi, solved_lo)
        + contract_rows(rhs_lo, solved_hi)
    )
    schur_update = schur[:mesh_width, :mesh_width]
    lateral_block = schur[mesh_width:, :mesh_width]
    apex_schur_block = schur[mesh_width:, mesh_width:]
    return (schur_update, lateral_block, apex_schur_block)


def local(hyper, spatial_prec, part_lengths, reading_index, reading_value, reading_cov):
    packed = jnp.concatenate(
        [reading_index.astype(jnp.float32), reading_value, reading_cov], axis=0
    )
    packed = lax.all_to_all(packed, "tm", split_axis=2, concat_axis=1, tiled=True)
    mesh_width = spatial_prec.shape[0]
    covars = reading_cov.shape[0]
    partition_position = lax.axis_index("tm")
    corr_time = hyper[0]
    tau_field = hyper[1]
    tau_fixed = hyper[2]
    prior_diag = (1.0 + corr_time * corr_time) * tau_field * spatial_prec
    coupling_block = -corr_time * tau_field * spatial_prec
    part_ends = (jnp.cumsum(part_lengths) - 1).astype(jnp.int32)
    my_end = part_ends[partition_position]
    local_length = part_lengths[partition_position]
    hessian, border, tip_data = assemble(packed, my_end, mesh_width, covars)

    def bypass_elimination():
        return (
            jnp.zeros_like(coupling_block),
            jnp.zeros((covars, mesh_width), coupling_block.dtype),
            jnp.zeros((covars, covars), coupling_block.dtype),
        )

    def perform_elimination():
        return eliminate(hessian, border, prior_diag, coupling_block)

    schur_update, lateral_block, apex_schur_block = lax.cond(
        local_length == 2, perform_elimination, bypass_elimination
    )
    has_left = partition_position > 0
    fill = jnp.where(has_left, jnp.where(local_length == 2, schur_update, coupling_block), 0.0)
    left_update = jnp.where(has_left, schur_update, 0.0)
    left_side = jnp.where(has_left, lateral_block, 0.0)
    packed_update = lower_blocks(left_update)
    packed_update, from_right_side = passed_along((packed_update, left_side), "tm", -1)
    from_right = from_lower_blocks(packed_update, mesh_width)
    sep_block = hessian[0] + prior_diag + schur_update + from_right
    sep_border = border[0] + lateral_block + from_right_side
    tip_total = butterfly_sum(tip_data + apex_schur_block, "tm")
    tip = tip_total + tau_fixed * jnp.eye(covars, dtype=jnp.float32)
    return (sep_block[None], fill[None], sep_border[None], tip)


def solution(mesh):
    in_specs = (
        P("groups"),
        P(),
        P("groups"),
        P(None, ("groups", "tm"), None),
        P(None, ("groups", "tm"), None),
        P(None, ("groups", "tm"), None),
    )
    out_specs = (
        P(("groups", "tm"), None, None),
        P(("groups", "tm"), None, None),
        P(("groups", "tm"), None, None),
        P("groups", None),
    )
    return jax.shard_map(local, mesh=mesh, in_specs=in_specs, out_specs=out_specs, check_vma=False)
```
